128 devices in a mesh: tm: 16 (over z_hi, y, core), tensor: 8 (over z_lo, x).
Axes of the slice: x: 4, y: 4, z: 4 (z_hi: 2, z_lo: 2; z = z_hi * 2 + z_lo), core: 2. Of those that a mesh axis runs over, the one named last changes fastest.
Arguments:
- hidden_in: bfloat16 [16, 2, 256, 5120], P('tm', None, None, 'tensor'), may hold values from -6 to 6
- noisy_queries: bfloat16 [16, 2, 256, 5120], P('tm', None, None, 'tensor'), may hold values from -28 to 28
- noisy_keys: bfloat16 [16, 2, 256, 5120], P('tm', None, None, 'tensor'), may hold values from -5 to 5
- noisy_values: bfloat16 [16, 2, 256, 5120], P('tm', None, None, 'tensor'), may hold values from -15 to 15
- clean_cache: bfloat16 [16, 2, 256, 5120], P('tm', None, None, 'tensor'), may hold values from -9 to 9
- out_proj: bfloat16 [5120, 5120], P('tensor'), may hold values from -0.078125 to 0.078125
- branch_in: bfloat16 [5120, 2560], P(None, 'tensor'), may hold values from -0.078125 to 0.078125
- branch_out: bfloat16 [2560, 5120], P('tensor'), may hold values from -0.125 to 0.125
- action_table: bfloat16 [128, 2560], P(None, 'tensor'), may hold values from -6 to 6
- actions: int32 [16, 4], P('tm'), may hold values from 0 to 127
- offsets: int32 [16], P('tm'), may hold values from 0 to 2, as said below
- out_grad: bfloat16 [16, 2, 256, 5120], P('tm', None, None, 'tensor'), may hold values from -6 to 6
Outputs:
- layer_out: bfloat16 [16, 2, 256, 5120], P('tm', None, None, 'tensor')
- input_grad: bfloat16 [16, 2, 256, 5120], P('tm', None, None, 'tensor')
- query_grad: bfloat16 [16, 2, 256, 5120], P('tm', None, None, 'tensor')
- key_grad: bfloat16 [16, 2, 256, 5120], P('tm', None, None, 'tensor')
- value_grad: bfloat16 [16, 2, 256, 5120], P('tm', None, None, 'tensor')
- cache_grad: float32 [16, 2, 256, 5120], P('tm', None, None, 'tensor')
- proj_weight_grad: float32 [5120, 5120], P('tensor', 'tm')
- branch_in_grad: float32 [5120, 2560], P('tm', 'tensor')
- branch_out_grad: float32 [2560, 5120], P('tensor', 'tm')
- table_grad: float32 [128, 2560], P('tm', 'tensor')
The draws below stay inside these ranges and needn't reach their ends.
Inputs may be any that keep to these rules, and one draw needn't show every extreme that they name: offsets[c] <= c; spans 1, 2, 7, 8, 9 and the last reach min(c, 2).
All inputs are finite; a program needn't handle non-finite values.
Results may differ from the reference program's by a relative error of at most 0.013.
Values may be sent and summed in bfloat16 or wider, within the bound.
No kernel may reach another device: no remote copies, remote signals or barrier semaphores. Data moves between devices by JAX's collectives and lax.ppermute only.
A program may use at most 192 MiB of HBM per device.

```python
import math
import jax
import jax.numpy as jnp
import numpy as np
from jax import lax

D = 5120
HEADS = 40
HD = 128
FA = 2560
NACT = 128
ACTS = 4
STEPS = 2
TOKC = 256
SPANS = 16
N_TENSOR = 8


def noisy_pair(key):
    shape = (SPANS, STEPS, TOKC, HEADS * HD)
    base_keys = jnp.clip(jax.random.normal(jax.random.fold_in(key, 7), shape, jnp.float32), -5.0, 5.0)
    base_queries = jnp.clip(jax.random.normal(jax.random.fold_in(key, 8), shape, jnp.float32), -5.0, 5.0)
    return (base_queries, base_keys)


def draw_noisy_queries(key, part):
    pair = noisy_pair(key)
    return pair[0].astype(jnp.bfloat16)


def draw_noisy_keys(key, part):
    pair = noisy_pair(key)
    return pair[1].astype(jnp.bfloat16)


def draw_offsets(key, part):
    positions = jnp.arange(SPANS)
    raw_reach = jax.random.randint(jax.random.fold_in(key, 21), (SPANS,), 0, 3)
    middle = SPANS // 2
    forced = (positions == 1) | (positions == 2) | (positions == SPANS - 1) | (jnp.abs(positions - middle) <= 1)
    raw_reach = jnp.where(forced, 2, raw_reach)
    return jnp.minimum(raw_reach, positions).astype(jnp.int32)


def with_ends(drawn, own_key, least, high):
    longest = drawn.shape.index(max(drawn.shape))
    spots = []
    for shift in (0, 1):
        where = [jax.random.randint(jax.random.fold_in(own_key, axis), (), 0, length) for axis, length in enumerate(drawn.shape)]
        where[longest] = (where[longest] + shift) % drawn.shape[longest]
        spots.append(tuple(where))
    return drawn.at[spots[0]].set(least).at[spots[1]].set(high)


def steps_of(own_key, extent, cuts, least, high):
    loudness = 1.0
    for axis_at, shards_of in cuts:
        heights = jax.random.uniform(jax.random.fold_in(jax.random.fold_in(own_key, 6), axis_at), (shards_of,), jnp.float32, least / len(cuts), high / len(cuts))
        loudness = loudness * jnp.repeat(jnp.exp(heights), extent[axis_at] // shards_of).reshape((-1,) + (1,) * (len(extent) - 1 - axis_at))
    return loudness


def rank_bounds(number_of, lean):
    portions = [(1 << 20) // math.isqrt(standing ** lean) + 1 for standing in range(1, number_of + 1)]
    spread = 1 + sum(portions) // (1 << 30)
    return np.cumsum(np.array([max(1, weight // spread) for weight in portions]))


def ranked(stream_key, dims, count, slope):
    table = rank_bounds(count, slope)
    pick = jax.random.randint(jax.random.fold_in(stream_key, 1), dims, 0, int(table[count - 1]))
    rank = jnp.searchsorted(jnp.asarray(table, jnp.int32), pick, side="right")
    return jax.random.permutation(jax.random.fold_in(stream_key, 2), count)[rank].astype(jnp.int32)


def bell_draw(own_key, shape, spread, limit, split=(), dtype=jnp.bfloat16):
    drawn = jax.random.normal(own_key, shape, jnp.float32) * spread
    if len(split) > 0:
        drawn = steps_of(own_key, shape, split, -0.22, 0.18) * drawn
    return jnp.clip(drawn, min=-limit, max=limit).astype(dtype)


def setup_inputs(seed: int = 0) -> dict:
    streams_of = jax.random.split(jax.random.key(seed), 13)
    return {
        "hidden_in": bell_draw(streams_of[0], (SPANS, STEPS, TOKC, D), 1.0, 6.0, ((0, 16), (3, 8))),
        "noisy_queries": draw_noisy_queries(jax.random.fold_in(streams_of[12], 71), 0),
        "noisy_keys": draw_noisy_keys(jax.random.fold_in(streams_of[12], 71), 0),
        "noisy_values": bell_draw(streams_of[3], (SPANS, STEPS, TOKC, HEADS * HD), 3.0, 15.0, ((0, 16), (3, 8))),
        "clean_cache": bell_draw(streams_of[4], (SPANS, 2, TOKC, HEADS * HD), 1.5, 9.0, ((0, 16), (3, 8))),
        "out_proj": bell_draw(streams_of[5], (HEADS * HD, D), (HEADS * HD) ** -0.5, 0.078125, ((0, 8),)),
        "branch_in": bell_draw(streams_of[6], (D, FA), D ** -0.5, 0.078125, ((1, 8),)),
        "branch_out": bell_draw(streams_of[7], (FA, D), FA ** -0.5, 0.125, ((0, 8),)),
        "action_table": bell_draw(streams_of[8], (NACT, FA), 1.0, 6.0, ((1, 8),)),
        "actions": with_ends(ranked(streams_of[9], (SPANS, ACTS), NACT, 2), jax.random.fold_in(streams_of[9], 3), 0, NACT - 1).astype(jnp.int32),
        "offsets": draw_offsets(jax.random.fold_in(streams_of[12], 71), 0),
        "out_grad": bell_draw(streams_of[11], (SPANS, STEPS, TOKC, D), 1.0, 6.0, ((0, 16), (3, 8))),
    }


GELU_C = 0.7978845608028654
GELU_A = 0.044715


def gelu_value(inputs):
    inner = GELU_C * (inputs + GELU_A * inputs * inputs * inputs)
    return 0.5 * inputs * (1.0 + jnp.tanh(inner))


def gelu_slope(inputs):
    tangent = jnp.tanh(GELU_C * (inputs + GELU_A * inputs * inputs * inputs))
    return 0.5 * (1.0 + tangent) + 0.5 * inputs * (1.0 - tangent * tangent) * GELU_C * (1.0 + 3.0 * GELU_A * inputs * inputs)


def reference(hidden_in, noisy_queries, noisy_keys, noisy_values, clean_cache, out_proj, branch_in, branch_out, action_table, actions, offsets, out_grad):
    head_width = HEADS * HD
    head_group = head_width // N_TENSOR
    branch_group = FA // N_TENSOR
    score_scale = HD ** -0.5
    row_count = STEPS * TOKC
    cache_terms = [jnp.zeros((2, TOKC, head_width), jnp.float32) for span_index in range(SPANS)]
    layer_list, input_list, query_list, key_list, value_list = [], [], [], [], []
    proj_sum = jnp.zeros((head_width, D), jnp.float32)
    in_sum = jnp.zeros((D, FA), jnp.float32)
    out_sum = jnp.zeros((FA, D), jnp.float32)
    table_sum = jnp.zeros((NACT, FA), jnp.float32)
    for span_index in range(SPANS):
        farther = clean_cache[max(span_index - 2, 0)]
        nearer = clean_cache[max(span_index - 1, 0)]
        reach = offsets[span_index]
        allowed = jnp.concatenate([jnp.full((TOKC,), reach >= 2), jnp.full((TOKC,), reach >= 1), jnp.ones((TOKC,), bool)])
        key_block = jnp.concatenate([jnp.broadcast_to(farther[0], (STEPS, TOKC, head_width)), jnp.broadcast_to(nearer[0], (STEPS, TOKC, head_width)), noisy_keys[span_index]], axis=1)
        value_block = jnp.concatenate([jnp.broadcast_to(farther[1], (STEPS, TOKC, head_width)), jnp.broadcast_to(nearer[1], (STEPS, TOKC, head_width)), noisy_values[span_index]], axis=1)
        query_heads = noisy_queries[span_index].reshape(STEPS, TOKC, HEADS, HD).astype(jnp.float32)
        key_heads = key_block.reshape(STEPS, 3 * TOKC, HEADS, HD).astype(jnp.float32)
        value_heads = value_block.reshape(STEPS, 3 * TOKC, HEADS, HD).astype(jnp.float32)
        scores = jnp.einsum("sqhe,skhe->shqk", query_heads, key_heads) * score_scale
        masked = jnp.where(allowed[None, None, None, :], scores, -1e30)
        largest = jnp.max(masked, axis=-1, keepdims=True)
        raised = jnp.exp(masked - largest)
        probs = raised / jnp.sum(raised, axis=-1, keepdims=True)
        probs_low = probs.astype(jnp.bfloat16)
        attended = jnp.einsum("shqk,skhe->sqhe", probs_low.astype(jnp.float32), value_heads).astype(jnp.bfloat16).reshape(row_count, head_width)
        input_rows = hidden_in[span_index].reshape(row_count, D)
        grad_rows = out_grad[span_index].reshape(row_count, D)
        onehot = (actions[span_index][:, None] == jnp.arange(NACT)[None, :]).astype(jnp.bfloat16)
        action_rows = jnp.dot(onehot, action_table, preferred_element_type=jnp.float32)
        pre_act = jnp.dot(input_rows, branch_in, preferred_element_type=jnp.float32).reshape(STEPS, ACTS, TOKC // ACTS, FA) + action_rows[None, :, None, :]
        pre_act = pre_act.reshape(row_count, FA)
        branch_act = gelu_value(pre_act).astype(jnp.bfloat16)
        layer_total = jnp.zeros((row_count, D), jnp.float32)
        input_total = jnp.zeros((row_count, D), jnp.float32)
        attended_grad = jnp.dot(grad_rows, out_proj.T, preferred_element_type=jnp.float32).astype(jnp.bfloat16)
        pre_grad = (jnp.dot(grad_rows, branch_out.T, preferred_element_type=jnp.float32) * gelu_slope(pre_act)).astype(jnp.bfloat16)
        for group_index in range(N_TENSOR):
            head_cols = slice(group_index * head_group, (group_index + 1) * head_group)
            branch_cols = slice(group_index * branch_group, (group_index + 1) * branch_group)
            partial_value = jnp.dot(attended[:, head_cols], out_proj[head_cols], preferred_element_type=jnp.float32) + jnp.dot(branch_act[:, branch_cols], branch_out[branch_cols], preferred_element_type=jnp.float32)
            layer_total = layer_total + partial_value.astype(jnp.bfloat16).astype(jnp.float32)
            back_part = jnp.dot(pre_grad[:, branch_cols], branch_in[:, branch_cols].T, preferred_element_type=jnp.float32)
            input_total = input_total + back_part.astype(jnp.bfloat16).astype(jnp.float32)
        layer_list.append((input_rows.astype(jnp.float32) + layer_total).astype(jnp.bfloat16).reshape(STEPS, TOKC, D))
        input_list.append((grad_rows.astype(jnp.float32) + input_total).astype(jnp.bfloat16).reshape(STEPS, TOKC, D))
        proj_sum = proj_sum + jnp.dot(attended.T, grad_rows, preferred_element_type=jnp.float32).astype(jnp.bfloat16).astype(jnp.float32)
        in_sum = in_sum + jnp.dot(input_rows.T, pre_grad, preferred_element_type=jnp.float32).astype(jnp.bfloat16).astype(jnp.float32)
        out_sum = out_sum + jnp.dot(branch_act.T, grad_rows, preferred_element_type=jnp.float32).astype(jnp.bfloat16).astype(jnp.float32)
        grouped = jnp.sum(pre_grad.reshape(STEPS, ACTS, TOKC // ACTS, FA).astype(jnp.float32), axis=(0, 2))
        table_term = jnp.dot(onehot.astype(jnp.float32).T, grouped, precision=lax.Precision.HIGHEST)
        table_sum = table_sum + table_term.astype(jnp.bfloat16).astype(jnp.float32)
        grad_heads = attended_grad.reshape(STEPS, TOKC, HEADS, HD).astype(jnp.float32)
        value_all = jnp.einsum("shqk,sqhe->skhe", probs_low.astype(jnp.float32), grad_heads)
        prob_grad = jnp.einsum("sqhe,skhe->shqk", grad_heads, value_heads)
        centre = jnp.sum(prob_grad * probs, axis=-1, keepdims=True)
        score_grad = (probs * (prob_grad - centre) * score_scale).astype(jnp.bfloat16)
        query_list.append(jnp.einsum("shqk,skhe->sqhe", score_grad.astype(jnp.float32), key_heads).astype(jnp.bfloat16).reshape(STEPS, TOKC, head_width))
        key_all = jnp.einsum("shqk,sqhe->skhe", score_grad.astype(jnp.float32), query_heads).reshape(STEPS, 3 * TOKC, head_width)
        value_all = value_all.reshape(STEPS, 3 * TOKC, head_width)
        key_list.append(key_all[:, 2 * TOKC:].astype(jnp.bfloat16))
        value_list.append(value_all[:, 2 * TOKC:].astype(jnp.bfloat16))
        if span_index >= 2:
            toward_far = jnp.stack([jnp.sum(key_all[:, :TOKC], axis=0), jnp.sum(value_all[:, :TOKC], axis=0)])
            cache_terms[span_index - 2] = cache_terms[span_index - 2] + toward_far
        if span_index >= 1:
            toward_near = jnp.stack([jnp.sum(key_all[:, TOKC:2 * TOKC], axis=0), jnp.sum(value_all[:, TOKC:2 * TOKC], axis=0)])
            cache_terms[span_index - 1] = cache_terms[span_index - 1] + toward_near
    return (jnp.stack(layer_list), jnp.stack(input_list), jnp.stack(query_list), jnp.stack(key_list), jnp.stack(value_list), jnp.stack(cache_terms), proj_sum, in_sum, out_sum, table_sum)
```

```python
import jax
import jax.numpy as jnp
from jax import lax
from jax.sharding import PartitionSpec as P

HD = 128


GELU_C = 0.7978845608028654
GELU_A = 0.044715


def from_behind(value, axis, steps):
    count = lax.axis_size(axis)
    first, last = (max(0, -steps), min(count, count - steps))
    return lax.ppermute(value, axis, [(source, source + steps) for source in range(first, last)])


def gelu_value(inputs):
    inner = GELU_C * (inputs + GELU_A * inputs * inputs * inputs)
    return 0.5 * inputs * (1.0 + jnp.tanh(inner))


def gelu_slope(inputs):
    tangent = jnp.tanh(GELU_C * (inputs + GELU_A * inputs * inputs * inputs))
    return 0.5 * (1.0 + tangent) + 0.5 * inputs * (1.0 - tangent * tangent) * GELU_C * (
        1.0 + 3.0 * GELU_A * inputs * inputs
    )


def contract_rows(left, right):
    return lax.dot_general(
        left, right, (((0,), (0,)), ((), ())), preferred_element_type=jnp.float32
    )


def contract_cols(left, right):
    return lax.dot_general(
        left, right, (((1,), (1,)), ((), ())), preferred_element_type=jnp.float32
    )


def body(
    hidden_in,
    noisy_queries,
    noisy_keys,
    noisy_values,
    clean_cache,
    out_proj,
    branch_in,
    branch_out,
    action_table,
    actions,
    offsets,
    out_grad,
):
    steps_here = noisy_queries.shape[1]
    tokens_here = noisy_queries.shape[2]
    head_width = noisy_queries.shape[3]
    heads_here = head_width // HD
    model_width = out_proj.shape[1]
    row_count = steps_here * tokens_here
    action_count = actions.shape[1]
    score_scale = HD ** (-0.5)
    full_both = lax.all_gather(
        jnp.concatenate([hidden_in, out_grad], axis=0), "tensor", axis=3, tiled=True
    )
    input_rows = full_both[0].reshape(row_count, model_width)
    grad_rows = full_both[1].reshape(row_count, model_width)
    own_cache = clean_cache[0]
    nearer = from_behind(own_cache, "tm", 1)
    farther = from_behind(own_cache, "tm", 2)
    reach = offsets[0]
    allowed = jnp.concatenate(
        [
            jnp.full((tokens_here,), reach >= 2),
            jnp.full((tokens_here,), reach >= 1),
            jnp.ones((tokens_here,), bool),
        ]
    )
    block_shape = (steps_here, tokens_here, head_width)
    key_block = jnp.concatenate(
        [
            jnp.broadcast_to(farther[0], block_shape),
            jnp.broadcast_to(nearer[0], block_shape),
            noisy_keys[0],
        ],
        axis=1,
    )
    value_block = jnp.concatenate(
        [
            jnp.broadcast_to(farther[1], block_shape),
            jnp.broadcast_to(nearer[1], block_shape),
            noisy_values[0],
        ],
        axis=1,
    )
    query_heads = noisy_queries[0].reshape(steps_here, tokens_here, heads_here, HD)
    key_heads = key_block.reshape(steps_here, 3 * tokens_here, heads_here, HD)
    value_heads = value_block.reshape(steps_here, 3 * tokens_here, heads_here, HD)
    scores = (
        jnp.einsum("sqhe,skhe->shqk", query_heads, key_heads, preferred_element_type=jnp.float32)
        * score_scale
    )
    masked = jnp.where(allowed[None, None, None, :], scores, -1e30)
    largest = jnp.max(masked, axis=-1, keepdims=True)
    raised = jnp.exp(masked - largest)
    probs = raised / jnp.sum(raised, axis=-1, keepdims=True)
    probs_low = probs.astype(jnp.bfloat16)
    attended = (
        jnp.einsum("shqk,skhe->sqhe", probs_low, value_heads, preferred_element_type=jnp.float32)
        .astype(jnp.bfloat16)
        .reshape(row_count, head_width)
    )
    onehot = (actions[0][:, None] == jnp.arange(action_table.shape[0])[None, :]).astype(
        jnp.bfloat16
    )
    action_rows = jnp.dot(onehot, action_table, preferred_element_type=jnp.float32)
    branch_width = branch_in.shape[1]
    pre_act = (
        jnp.dot(input_rows, branch_in, preferred_element_type=jnp.float32).reshape(
            steps_here, action_count, tokens_here // action_count, branch_width
        )
        + action_rows[None, :, None, :]
    )
    pre_act = pre_act.reshape(row_count, branch_width)
    branch_act = gelu_value(pre_act).astype(jnp.bfloat16)
    partial_value = jnp.dot(attended, out_proj, preferred_element_type=jnp.float32) + jnp.dot(
        branch_act, branch_out, preferred_element_type=jnp.float32
    )
    layer_sum = lax.psum_scatter(
        partial_value.reshape(1, steps_here, tokens_here, model_width).astype(jnp.bfloat16),
        "tensor",
        scatter_dimension=3,
        tiled=True,
    ).astype(jnp.float32)
    layer_out = (hidden_in.astype(jnp.float32) + layer_sum).astype(jnp.bfloat16)
    attended_grad = contract_cols(grad_rows, out_proj).astype(jnp.bfloat16)
    pre_grad = (contract_cols(grad_rows, branch_out) * gelu_slope(pre_act)).astype(jnp.bfloat16)
    tm_count = lax.axis_size("tm")
    col_block = model_width // tm_count
    grad_split = grad_rows.reshape(row_count, tm_count, col_block)
    in_term = jnp.einsum(
        "rjk,rn->jkn",
        input_rows.reshape(row_count, tm_count, model_width // tm_count),
        pre_grad,
        preferred_element_type=jnp.float32,
    )
    out_term = jnp.einsum("rk,rjn->jkn", branch_act, grad_split, preferred_element_type=jnp.float32)
    grouped = jnp.sum(
        pre_grad.reshape(
            steps_here, action_count, tokens_here // action_count, branch_width
        ).astype(jnp.float32),
        axis=(0, 2),
    )
    table_term = jnp.dot(onehot.astype(jnp.float32).T, grouped, precision=lax.Precision.HIGHEST)
    proj_term = jnp.einsum("rk,rjn->jkn", attended, grad_split, preferred_element_type=jnp.float32)
    table_rows = table_term.shape[0] // tm_count
    pieces = (
        proj_term.astype(jnp.bfloat16),
        in_term.astype(jnp.bfloat16),
        out_term.astype(jnp.bfloat16),
        table_term.reshape(tm_count, table_rows, branch_width).astype(jnp.bfloat16),
    )
    merged = lax.psum_scatter(
        jnp.concatenate(pieces, axis=1), "tm", scatter_dimension=0, tiled=True
    )[0].astype(jnp.float32)
    bounds = [0]
    for piece in pieces:
        bounds.append(bounds[-1] + piece.shape[1])
    summed = tuple(merged[bounds[i] : bounds[i + 1]] for i in range(4))
    input_term = contract_cols(pre_grad, branch_in)
    input_sum = lax.psum_scatter(
        input_term.reshape(1, steps_here, tokens_here, model_width).astype(jnp.bfloat16),
        "tensor",
        scatter_dimension=3,
        tiled=True,
    ).astype(jnp.float32)
    input_grad = (out_grad.astype(jnp.float32) + input_sum).astype(jnp.bfloat16)
    weight_grads = (summed, input_grad)
    grad_heads = attended_grad.reshape(steps_here, tokens_here, heads_here, HD)
    value_all = jnp.einsum(
        "shqk,sqhe->skhe", probs_low, grad_heads, preferred_element_type=jnp.float32
    )
    prob_grad = jnp.einsum(
        "sqhe,skhe->shqk", grad_heads, value_heads, preferred_element_type=jnp.float32
    )
    centre = jnp.sum(prob_grad * probs, axis=-1, keepdims=True)
    score_grad = (probs * (prob_grad - centre) * score_scale).astype(jnp.bfloat16)
    query_grad = (
        jnp.einsum("shqk,skhe->sqhe", score_grad, key_heads, preferred_element_type=jnp.float32)
        .astype(jnp.bfloat16)
        .reshape(1, steps_here, tokens_here, head_width)
    )
    key_all = jnp.einsum(
        "shqk,sqhe->skhe", score_grad, query_heads, preferred_element_type=jnp.float32
    ).reshape(steps_here, 3 * tokens_here, head_width)
    value_all = value_all.reshape(steps_here, 3 * tokens_here, head_width)
    own_key = key_all[:, 2 * tokens_here :].astype(jnp.bfloat16)[None]
    own_value = value_all[:, 2 * tokens_here :].astype(jnp.bfloat16)[None]
    toward_far = jnp.stack(
        [jnp.sum(key_all[:, :tokens_here], axis=0), jnp.sum(value_all[:, :tokens_here], axis=0)]
    )
    toward_near = jnp.stack(
        [
            jnp.sum(key_all[:, tokens_here : 2 * tokens_here], axis=0),
            jnp.sum(value_all[:, tokens_here : 2 * tokens_here], axis=0),
        ]
    )
    from_next = from_behind(toward_near.astype(jnp.bfloat16), "tm", -1).astype(toward_near.dtype)
    from_after = from_behind(toward_far.astype(jnp.bfloat16), "tm", -2).astype(toward_far.dtype)
    received = from_next + from_after
    attention_grads = (query_grad, own_key, own_value, received[None])
    summed, input_grad = weight_grads
    query_grad, own_key, own_value, cache_grad = attention_grads
    return (
        layer_out,
        input_grad,
        query_grad,
        own_key,
        own_value,
        cache_grad,
        summed[0],
        summed[1],
        summed[2],
        summed[3],
    )


def solution(mesh):
    in_specs = (
        P("tm", None, None, "tensor"),
        P("tm", None, None, "tensor"),
        P("tm", None, None, "tensor"),
        P("tm", None, None, "tensor"),
        P("tm", None, None, "tensor"),
        P("tensor", None),
        P(None, "tensor"),
        P("tensor", None),
        P(None, "tensor"),
        P("tm", None),
        P("tm"),
        P("tm", None, None, "tensor"),
    )
    out_specs = (
        P("tm", None, None, "tensor"),
        P("tm", None, None, "tensor"),
        P("tm", None, None, "tensor"),
        P("tm", None, None, "tensor"),
        P("tm", None, None, "tensor"),
        P("tm", None, None, "tensor"),
        P("tensor", "tm"),
        P("tm", "tensor"),
        P("tensor", "tm"),
        P("tm", "tensor"),
    )
    return jax.shard_map(body, mesh=mesh, in_specs=in_specs, out_specs=out_specs, check_vma=False)
```

```python
import jax
import jax.numpy as jnp
from jax import lax
from jax.sharding import PartitionSpec as P

HD = 128


GELU_C = 0.7978845608028654
GELU_A = 0.044715


def from_behind(value, axis, steps):
    count = lax.axis_size(axis)
    first, last = (max(0, -steps), min(count, count - steps))
    return lax.ppermute(value, axis, [(source, source + steps) for source in range(first, last)])


def gelu_value(inputs):
    inner = GELU_C * (inputs + GELU_A * inputs * inputs * inputs)
    return 0.5 * inputs * (1.0 + jnp.tanh(inner))


def gelu_slope(inputs):
    tangent = jnp.tanh(GELU_C * (inputs + GELU_A * inputs * inputs * inputs))
    return 0.5 * (1.0 + tangent) + 0.5 * inputs * (1.0 - tangent * tangent) * GELU_C * (
        1.0 + 3.0 * GELU_A * inputs * inputs
    )


def contract_rows(left, right):
    return lax.dot_general(
        left, right, (((0,), (0,)), ((), ())), preferred_element_type=jnp.float32
    )


def contract_cols(left, right):
    return lax.dot_general(
        left, right, (((1,), (1,)), ((), ())), preferred_element_type=jnp.float32
    )


def sum_over_groups(partial, steps_here, tokens_here):
    count = lax.axis_size("tensor")
    rows, width = partial.shape
    blocks = partial.reshape(rows, count, width // count)
    received = lax.all_to_all(blocks, "tensor", 1, 1, tiled=True)
    total = jnp.sum(received.astype(jnp.float32), axis=1)
    return total.reshape(1, steps_here, tokens_here, width // count)


def body(
    hidden_in,
    noisy_queries,
    noisy_keys,
    noisy_values,
    clean_cache,
    out_proj,
    branch_in,
    branch_out,
    action_table,
    actions,
    offsets,
    out_grad,
):
    steps_here = noisy_queries.shape[1]
    tokens_here = noisy_queries.shape[2]
    head_width = noisy_queries.shape[3]
    heads_here = head_width // HD
    model_width = out_proj.shape[1]
    row_count = steps_here * tokens_here
    action_count = actions.shape[1]
    score_scale = HD ** (-0.5)
    full_both = lax.all_gather(
        jnp.concatenate([hidden_in, out_grad], axis=0), "tensor", axis=3, tiled=True
    )
    input_rows = full_both[0].reshape(row_count, model_width)
    grad_rows = full_both[1].reshape(row_count, model_width)
    own_cache = clean_cache[0]
    nearer = from_behind(own_cache, "tm", 1)
    farther = from_behind(own_cache, "tm", 2)
    reach = offsets[0]
    allowed = jnp.concatenate(
        [
            jnp.full((tokens_here,), reach >= 2),
            jnp.full((tokens_here,), reach >= 1),
            jnp.ones((tokens_here,), bool),
        ]
    )
    block_shape = (steps_here, tokens_here, head_width)
    key_block = jnp.concatenate(
        [
            jnp.broadcast_to(farther[0], block_shape),
            jnp.broadcast_to(nearer[0], block_shape),
            noisy_keys[0],
        ],
        axis=1,
    )
    value_block = jnp.concatenate(
        [
            jnp.broadcast_to(farther[1], block_shape),
            jnp.broadcast_to(nearer[1], block_shape),
            noisy_values[0],
        ],
        axis=1,
    )
    query_heads = noisy_queries[0].reshape(steps_here, tokens_here, heads_here, HD)
    key_heads = key_block.reshape(steps_here, 3 * tokens_here, heads_here, HD)
    value_heads = value_block.reshape(steps_here, 3 * tokens_here, heads_here, HD)
    scores = (
        jnp.einsum("sqhe,skhe->shqk", query_heads, key_heads, preferred_element_type=jnp.float32)
        * score_scale
    )
    masked = jnp.where(allowed[None, None, None, :], scores, -1e30)
    largest = jnp.max(masked, axis=-1, keepdims=True)
    raised = jnp.exp(masked - largest)
    probs = raised / jnp.sum(raised, axis=-1, keepdims=True)
    probs_low = probs.astype(jnp.bfloat16)
    attended = (
        jnp.einsum("shqk,skhe->sqhe", probs_low, value_heads, preferred_element_type=jnp.float32)
        .astype(jnp.bfloat16)
        .reshape(row_count, head_width)
    )
    onehot = (actions[0][:, None] == jnp.arange(action_table.shape[0])[None, :]).astype(
        jnp.bfloat16
    )
    action_rows = jnp.dot(onehot, action_table, preferred_element_type=jnp.float32)
    branch_width = branch_in.shape[1]
    pre_act = (
        jnp.dot(input_rows, branch_in, preferred_element_type=jnp.float32).reshape(
            steps_here, action_count, tokens_here // action_count, branch_width
        )
        + action_rows[None, :, None, :]
    )
    pre_act = pre_act.reshape(row_count, branch_width)
    branch_act = gelu_value(pre_act).astype(jnp.bfloat16)
    partial_value = jnp.dot(attended, out_proj, preferred_element_type=jnp.float32) + jnp.dot(
        branch_act, branch_out, preferred_element_type=jnp.float32
    )
    layer_sum = sum_over_groups(partial_value.astype(jnp.bfloat16), steps_here, tokens_here)
    layer_out = (hidden_in.astype(jnp.float32) + layer_sum).astype(jnp.bfloat16)
    attended_grad = contract_cols(grad_rows, out_proj).astype(jnp.bfloat16)
    pre_grad = (contract_cols(grad_rows, branch_out) * gelu_slope(pre_act)).astype(jnp.bfloat16)
    tm_count = lax.axis_size("tm")
    col_block = model_width // tm_count
    grad_split = grad_rows.reshape(row_count, tm_count, col_block)
    in_term = jnp.einsum(
        "rjk,rn->jkn",
        input_rows.reshape(row_count, tm_count, model_width // tm_count),
        pre_grad,
        preferred_element_type=jnp.float32,
    )
    out_term = jnp.einsum("rk,rjn->jkn", branch_act, grad_split, preferred_element_type=jnp.float32)
    grouped = jnp.sum(
        pre_grad.reshape(
            steps_here, action_count, tokens_here // action_count, branch_width
        ).astype(jnp.float32),
        axis=(0, 2),
    )
    table_term = jnp.dot(onehot.astype(jnp.float32).T, grouped, precision=lax.Precision.HIGHEST)
    proj_term = jnp.einsum("rk,rjn->jkn", attended, grad_split, preferred_element_type=jnp.float32)
    table_rows = table_term.shape[0] // tm_count
    pieces = (
        proj_term.astype(jnp.bfloat16),
        in_term.astype(jnp.bfloat16),
        out_term.astype(jnp.bfloat16),
        table_term.reshape(tm_count, table_rows, branch_width).astype(jnp.bfloat16),
    )
    merged = lax.psum_scatter(
        jnp.concatenate(pieces, axis=1), "tm", scatter_dimension=0, tiled=True
    )[0].astype(jnp.float32)
    bounds = [0]
    for piece in pieces:
        bounds.append(bounds[-1] + piece.shape[1])
    summed = tuple(merged[bounds[i] : bounds[i + 1]] for i in range(4))
    input_term = contract_cols(pre_grad, branch_in)
    input_sum = sum_over_groups(input_term.astype(jnp.bfloat16), steps_here, tokens_here)
    input_grad = (out_grad.astype(jnp.float32) + input_sum).astype(jnp.bfloat16)
    weight_grads = (summed, input_grad)
    grad_heads = attended_grad.reshape(steps_here, tokens_here, heads_here, HD)
    value_all = jnp.einsum(
        "shqk,sqhe->skhe", probs_low, grad_heads, preferred_element_type=jnp.float32
    )
    prob_grad = jnp.einsum(
        "sqhe,skhe->shqk", grad_heads, value_heads, preferred_element_type=jnp.float32
    )
    centre = jnp.sum(prob_grad * probs, axis=-1, keepdims=True)
    score_grad = (probs * (prob_grad - centre) * score_scale).astype(jnp.bfloat16)
    query_grad = (
        jnp.einsum("shqk,skhe->sqhe", score_grad, key_heads, preferred_element_type=jnp.float32)
        .astype(jnp.bfloat16)
        .reshape(1, steps_here, tokens_here, head_width)
    )
    key_all = jnp.einsum(
        "shqk,sqhe->skhe", score_grad, query_heads, preferred_element_type=jnp.float32
    ).reshape(steps_here, 3 * tokens_here, head_width)
    value_all = value_all.reshape(steps_here, 3 * tokens_here, head_width)
    own_key = key_all[:, 2 * tokens_here :].astype(jnp.bfloat16)[None]
    own_value = value_all[:, 2 * tokens_here :].astype(jnp.bfloat16)[None]
    toward_far = jnp.stack(
        [jnp.sum(key_all[:, :tokens_here], axis=0), jnp.sum(value_all[:, :tokens_here], axis=0)]
    )
    toward_near = jnp.stack(
        [
            jnp.sum(key_all[:, tokens_here : 2 * tokens_here], axis=0),
            jnp.sum(value_all[:, tokens_here : 2 * tokens_here], axis=0),
        ]
    )
    from_next = from_behind(toward_near.astype(jnp.bfloat16), "tm", -1).astype(toward_near.dtype)
    from_after = from_behind(toward_far.astype(jnp.bfloat16), "tm", -2).astype(toward_far.dtype)
    received = from_next + from_after
    attention_grads = (query_grad, own_key, own_value, received[None])
    summed, input_grad = weight_grads
    query_grad, own_key, own_value, cache_grad = attention_grads
    return (
        layer_out,
        input_grad,
        query_grad,
        own_key,
        own_value,
        cache_grad,
        summed[0],
        summed[1],
        summed[2],
        summed[3],
    )


def solution(mesh):
    in_specs = (
        P("tm", None, None, "tensor"),
        P("tm", None, None, "tensor"),
        P("tm", None, None, "tensor"),
        P("tm", None, None, "tensor"),
        P("tm", None, None, "tensor"),
        P("tensor", None),
        P(None, "tensor"),
        P("tensor", None),
        P(None, "tensor"),
        P("tm", None),
        P("tm"),
        P("tm", None, None, "tensor"),
    )
    out_specs = (
        P("tm", None, None, "tensor"),
        P("tm", None, None, "tensor"),
        P("tm", None, None, "tensor"),
        P("tm", None, None, "tensor"),
        P("tm", None, None, "tensor"),
        P("tm", None, None, "tensor"),
        P("tensor", "tm"),
        P("tm", "tensor"),
        P("tensor", "tm"),
        P("tm", "tensor"),
    )
    return jax.shard_map(body, mesh=mesh, in_specs=in_specs, out_specs=out_specs, check_vma=False)
```

```python
import jax
import jax.numpy as jnp
from jax import lax
from jax.sharding import PartitionSpec as P

HD = 128


GELU_C = 0.7978845608028654
GELU_A = 0.044715


def from_behind(value, axis, steps):
    count = lax.axis_size(axis)
    first, last = (max(0, -steps), min(count, count - steps))
    return lax.ppermute(value, axis, [(source, source + steps) for source in range(first, last)])


def gelu_value(inputs):
    inner = GELU_C * (inputs + GELU_A * inputs * inputs * inputs)
    return 0.5 * inputs * (1.0 + jnp.tanh(inner))


def gelu_slope(inputs):
    tangent = jnp.tanh(GELU_C * (inputs + GELU_A * inputs * inputs * inputs))
    return 0.5 * (1.0 + tangent) + 0.5 * inputs * (1.0 - tangent * tangent) * GELU_C * (
        1.0 + 3.0 * GELU_A * inputs * inputs
    )


def contract_rows(left, right):
    return lax.dot_general(
        left, right, (((0,), (0,)), ((), ())), preferred_element_type=jnp.float32
    )


def contract_cols(left, right):
    return lax.dot_general(
        left, right, (((1,), (1,)), ((), ())), preferred_element_type=jnp.float32
    )


def sum_over_groups(partial, steps_here, tokens_here):
    count = lax.axis_size("tensor")
    rows, width = partial.shape
    blocks = partial.reshape(rows, count, width // count)
    received = lax.all_to_all(blocks, "tensor", 1, 1, tiled=True)
    total = jnp.sum(received.astype(jnp.float32), axis=1)
    return total.reshape(1, steps_here, tokens_here, width // count)


def body(
    hidden_in,
    noisy_queries,
    noisy_keys,
    noisy_values,
    clean_cache,
    out_proj,
    branch_in,
    branch_out,
    action_table,
    actions,
    offsets,
    out_grad,
):
    steps_here = noisy_queries.shape[1]
    tokens_here = noisy_queries.shape[2]
    head_width = noisy_queries.shape[3]
    heads_here = head_width // HD
    model_width = out_proj.shape[1]
    row_count = steps_here * tokens_here
    action_count = actions.shape[1]
    score_scale = HD ** (-0.5)
    group_count = lax.axis_size("tensor")
    full_inputs = lax.all_gather(hidden_in, "tensor", axis=3, tiled=True)
    copies = jnp.broadcast_to(out_grad, (group_count,) + out_grad.shape[1:])
    gathered = lax.all_to_all(copies, "tensor", 0, 0, tiled=True)
    input_rows = full_inputs.reshape(row_count, model_width)
    grad_rows = jnp.transpose(gathered, (1, 2, 0, 3)).reshape(row_count, model_width)
    own_cache = clean_cache[0]
    nearer = from_behind(own_cache, "tm", 1)
    farther = from_behind(own_cache, "tm", 2)
    reach = offsets[0]
    allowed = jnp.concatenate(
        [
            jnp.full((tokens_here,), reach >= 2),
            jnp.full((tokens_here,), reach >= 1),
            jnp.ones((tokens_here,), bool),
        ]
    )
    block_shape = (steps_here, tokens_here, head_width)
    key_block = jnp.concatenate(
        [
            jnp.broadcast_to(farther[0], block_shape),
            jnp.broadcast_to(nearer[0], block_shape),
            noisy_keys[0],
        ],
        axis=1,
    )
    value_block = jnp.concatenate(
        [
            jnp.broadcast_to(farther[1], block_shape),
            jnp.broadcast_to(nearer[1], block_shape),
            noisy_values[0],
        ],
        axis=1,
    )
    query_heads = noisy_queries[0].reshape(steps_here, tokens_here, heads_here, HD)
    key_heads = key_block.reshape(steps_here, 3 * tokens_here, heads_here, HD)
    value_heads = value_block.reshape(steps_here, 3 * tokens_here, heads_here, HD)
    scores = (
        jnp.einsum("sqhe,skhe->shqk", query_heads, key_heads, preferred_element_type=jnp.float32)
        * score_scale
    )
    masked = jnp.where(allowed[None, None, None, :], scores, -1e30)
    largest = jnp.max(masked, axis=-1, keepdims=True)
    raised = jnp.exp(masked - largest)
    probs = raised / jnp.sum(raised, axis=-1, keepdims=True)
    probs_low = probs.astype(jnp.bfloat16)
    attended = (
        jnp.einsum("shqk,skhe->sqhe", probs_low, value_heads, preferred_element_type=jnp.float32)
        .astype(jnp.bfloat16)
        .reshape(row_count, head_width)
    )
    onehot = (actions[0][:, None] == jnp.arange(action_table.shape[0])[None, :]).astype(
        jnp.bfloat16
    )
    action_rows = jnp.dot(onehot, action_table, preferred_element_type=jnp.float32)
    branch_width = branch_in.shape[1]
    pre_act = (
        jnp.dot(input_rows, branch_in, preferred_element_type=jnp.float32).reshape(
            steps_here, action_count, tokens_here // action_count, branch_width
        )
        + action_rows[None, :, None, :]
    )
    pre_act = pre_act.reshape(row_count, branch_width)
    branch_act = gelu_value(pre_act).astype(jnp.bfloat16)
    partial_value = jnp.dot(attended, out_proj, preferred_element_type=jnp.float32) + jnp.dot(
        branch_act, branch_out, preferred_element_type=jnp.float32
    )
    layer_sum = sum_over_groups(partial_value.astype(jnp.bfloat16), steps_here, tokens_here)
    layer_out = (hidden_in.astype(jnp.float32) + layer_sum).astype(jnp.bfloat16)
    attended_grad = contract_cols(grad_rows, out_proj).astype(jnp.bfloat16)
    pre_grad = (contract_cols(grad_rows, branch_out) * gelu_slope(pre_act)).astype(jnp.bfloat16)
    tm_count = lax.axis_size("tm")
    col_block = model_width // tm_count
    grad_split = grad_rows.reshape(row_count, tm_count, col_block)
    in_term = jnp.einsum(
        "rjk,rn->jkn",
        input_rows.reshape(row_count, tm_count, model_width // tm_count),
        pre_grad,
        preferred_element_type=jnp.float32,
    )
    out_term = jnp.einsum("rk,rjn->jkn", branch_act, grad_split, preferred_element_type=jnp.float32)
    grouped = jnp.sum(
        pre_grad.reshape(
            steps_here, action_count, tokens_here // action_count, branch_width
        ).astype(jnp.float32),
        axis=(0, 2),
    )
    table_term = jnp.dot(onehot.astype(jnp.float32).T, grouped, precision=lax.Precision.HIGHEST)
    proj_term = jnp.einsum("rk,rjn->jkn", attended, grad_split, preferred_element_type=jnp.float32)
    table_rows = table_term.shape[0] // tm_count
    pieces = (
        proj_term.astype(jnp.bfloat16),
        in_term.astype(jnp.bfloat16),
        out_term.astype(jnp.bfloat16),
        table_term.reshape(tm_count, table_rows, branch_width).astype(jnp.bfloat16),
    )
    proj_sum = lax.psum_scatter(pieces[0], "tm", scatter_dimension=0, tiled=True)[0]
    merged = lax.psum_scatter(
        jnp.concatenate(pieces[1:], axis=1), "tm", scatter_dimension=0, tiled=True
    )[0]
    bounds = [0]
    for piece in pieces[1:]:
        bounds.append(bounds[-1] + piece.shape[1])
    summed = (proj_sum.astype(jnp.float32),) + tuple(
        merged[bounds[i] : bounds[i + 1]].astype(jnp.float32) for i in range(3)
    )
    input_term = contract_cols(pre_grad, branch_in)
    input_sum = sum_over_groups(input_term.astype(jnp.bfloat16), steps_here, tokens_here)
    input_grad = (out_grad.astype(jnp.float32) + input_sum).astype(jnp.bfloat16)
    weight_grads = (summed, input_grad)
    grad_heads = attended_grad.reshape(steps_here, tokens_here, heads_here, HD)
    value_all = jnp.einsum(
        "shqk,sqhe->skhe", probs_low, grad_heads, preferred_element_type=jnp.float32
    )
    prob_grad = jnp.einsum(
        "sqhe,skhe->shqk", grad_heads, value_heads, preferred_element_type=jnp.float32
    )
    centre = jnp.sum(prob_grad * probs, axis=-1, keepdims=True)
    score_grad = (probs * (prob_grad - centre) * score_scale).astype(jnp.bfloat16)
    query_grad = (
        jnp.einsum("shqk,skhe->sqhe", score_grad, key_heads, preferred_element_type=jnp.float32)
        .astype(jnp.bfloat16)
        .reshape(1, steps_here, tokens_here, head_width)
    )
    key_all = jnp.einsum(
        "shqk,sqhe->skhe", score_grad, query_heads, preferred_element_type=jnp.float32
    ).reshape(steps_here, 3 * tokens_here, head_width)
    value_all = value_all.reshape(steps_here, 3 * tokens_here, head_width)
    own_key = key_all[:, 2 * tokens_here :].astype(jnp.bfloat16)[None]
    own_value = value_all[:, 2 * tokens_here :].astype(jnp.bfloat16)[None]
    toward_far = jnp.stack(
        [jnp.sum(key_all[:, :tokens_here], axis=0), jnp.sum(value_all[:, :tokens_here], axis=0)]
    )
    toward_near = jnp.stack(
        [
            jnp.sum(key_all[:, tokens_here : 2 * tokens_here], axis=0),
            jnp.sum(value_all[:, tokens_here : 2 * tokens_here], axis=0),
        ]
    )
    from_next = from_behind(toward_near.astype(jnp.bfloat16), "tm", -1).astype(toward_near.dtype)
    from_after = from_behind(toward_far.astype(jnp.bfloat16), "tm", -2).astype(toward_far.dtype)
    received = from_next + from_after
    attention_grads = (query_grad, own_key, own_value, received[None])
    summed, input_grad = weight_grads
    query_grad, own_key, own_value, cache_grad = attention_grads
    return (
        layer_out,
        input_grad,
        query_grad,
        own_key,
        own_value,
        cache_grad,
        summed[0],
        summed[1],
        summed[2],
        summed[3],
    )


def solution(mesh):
    in_specs = (
        P("tm", None, None, "tensor"),
        P("tm", None, None, "tensor"),
        P("tm", None, None, "tensor"),
        P("tm", None, None, "tensor"),
        P("tm", None, None, "tensor"),
        P("tensor", None),
        P(None, "tensor"),
        P("tensor", None),
        P(None, "tensor"),
        P("tm", None),
        P("tm"),
        P("tm", None, None, "tensor"),
    )
    out_specs = (
        P("tm", None, None, "tensor"),
        P("tm", None, None, "tensor"),
        P("tm", None, None, "tensor"),
        P("tm", None, None, "tensor"),
        P("tm", None, None, "tensor"),
        P("tm", None, None, "tensor"),
        P("tensor", "tm"),
        P("tm", "tensor"),
        P("tensor", "tm"),
        P("tm", "tensor"),
    )
    return jax.shard_map(body, mesh=mesh, in_specs=in_specs, out_specs=out_specs, check_vma=False)
```

```python
import jax
import jax.numpy as jnp
from jax import lax
from jax.sharding import PartitionSpec as P

HD = 128


GELU_C = 0.7978845608028654
GELU_A = 0.044715


def from_behind(value, axis, steps):
    count = lax.axis_size(axis)
    first, last = (max(0, -steps), min(count, count - steps))
    return lax.ppermute(value, axis, [(source, source + steps) for source in range(first, last)])


def gelu_value(inputs):
    inner = GELU_C * (inputs + GELU_A * inputs * inputs * inputs)
    return 0.5 * inputs * (1.0 + jnp.tanh(inner))


def gelu_slope(inputs):
    tangent = jnp.tanh(GELU_C * (inputs + GELU_A * inputs * inputs * inputs))
    return 0.5 * (1.0 + tangent) + 0.5 * inputs * (1.0 - tangent * tangent) * GELU_C * (
        1.0 + 3.0 * GELU_A * inputs * inputs
    )


def contract_rows(left, right):
    return lax.dot_general(
        left, right, (((0,), (0,)), ((), ())), preferred_element_type=jnp.float32
    )


def contract_cols(left, right):
    return lax.dot_general(
        left, right, (((1,), (1,)), ((), ())), preferred_element_type=jnp.float32
    )


def sum_over_groups(partial, steps_here, tokens_here):
    count = lax.axis_size("tensor")
    rows, width = partial.shape
    blocks = partial.reshape(rows, count, width // count)
    received = lax.all_to_all(blocks, "tensor", 1, 1, tiled=True)
    total = jnp.sum(received.astype(jnp.float32), axis=1)
    return total.reshape(1, steps_here, tokens_here, width // count)


def body(
    hidden_in,
    noisy_queries,
    noisy_keys,
    noisy_values,
    clean_cache,
    out_proj,
    branch_in,
    branch_out,
    action_table,
    actions,
    offsets,
    out_grad,
):
    steps_here = noisy_queries.shape[1]
    tokens_here = noisy_queries.shape[2]
    head_width = noisy_queries.shape[3]
    heads_here = head_width // HD
    model_width = out_proj.shape[1]
    row_count = steps_here * tokens_here
    action_count = actions.shape[1]
    score_scale = HD ** (-0.5)
    full_both = lax.all_gather(
        jnp.concatenate([hidden_in, out_grad], axis=0), "tensor", axis=3, tiled=True
    )
    input_rows = full_both[0].reshape(row_count, model_width)
    grad_rows = full_both[1].reshape(row_count, model_width)
    own_cache = clean_cache[0]
    nearer = from_behind(own_cache, "tm", 1)
    farther = from_behind(own_cache, "tm", 2)
    reach = offsets[0]
    allowed = jnp.concatenate(
        [
            jnp.full((tokens_here,), reach >= 2),
            jnp.full((tokens_here,), reach >= 1),
            jnp.ones((tokens_here,), bool),
        ]
    )
    block_shape = (steps_here, tokens_here, head_width)
    key_block = jnp.concatenate(
        [
            jnp.broadcast_to(farther[0], block_shape),
            jnp.broadcast_to(nearer[0], block_shape),
            noisy_keys[0],
        ],
        axis=1,
    )
    value_block = jnp.concatenate(
        [
            jnp.broadcast_to(farther[1], block_shape),
            jnp.broadcast_to(nearer[1], block_shape),
            noisy_values[0],
        ],
        axis=1,
    )
    query_heads = noisy_queries[0].reshape(steps_here, tokens_here, heads_here, HD)
    key_heads = key_block.reshape(steps_here, 3 * tokens_here, heads_here, HD)
    value_heads = value_block.reshape(steps_here, 3 * tokens_here, heads_here, HD)
    scores = (
        jnp.einsum("sqhe,skhe->shqk", query_heads, key_heads, preferred_element_type=jnp.float32)
        * score_scale
    )
    masked = jnp.where(allowed[None, None, None, :], scores, -1e30)
    largest = jnp.max(masked, axis=-1, keepdims=True)
    raised = jnp.exp(masked - largest)
    probs = raised / jnp.sum(raised, axis=-1, keepdims=True)
    probs_low = probs.astype(jnp.bfloat16)
    attended = (
        jnp.einsum("shqk,skhe->sqhe", probs_low, value_heads, preferred_element_type=jnp.float32)
        .astype(jnp.bfloat16)
        .reshape(row_count, head_width)
    )
    onehot = (actions[0][:, None] == jnp.arange(action_table.shape[0])[None, :]).astype(
        jnp.bfloat16
    )
    action_rows = jnp.dot(onehot, action_table, preferred_element_type=jnp.float32)
    branch_width = branch_in.shape[1]
    pre_act = (
        jnp.dot(input_rows, branch_in, preferred_element_type=jnp.float32).reshape(
            steps_here, action_count, tokens_here // action_count, branch_width
        )
        + action_rows[None, :, None, :]
    )
    pre_act = pre_act.reshape(row_count, branch_width)
    branch_act = gelu_value(pre_act).astype(jnp.bfloat16)
    partial_value = jnp.dot(attended, out_proj, preferred_element_type=jnp.float32) + jnp.dot(
        branch_act, branch_out, preferred_element_type=jnp.float32
    )
    layer_sum = sum_over_groups(partial_value.astype(jnp.bfloat16), steps_here, tokens_here)
    layer_out = (hidden_in.astype(jnp.float32) + layer_sum).astype(jnp.bfloat16)
    attended_grad = contract_cols(grad_rows, out_proj).astype(jnp.bfloat16)
    pre_grad = (contract_cols(grad_rows, branch_out) * gelu_slope(pre_act)).astype(jnp.bfloat16)
    tm_count = lax.axis_size("tm")
    grouped = jnp.sum(
        pre_grad.reshape(
            steps_here, action_count, tokens_here // action_count, branch_width
        ).astype(jnp.float32),
        axis=(0, 2),
    )
    table_term = jnp.dot(onehot.astype(jnp.float32).T, grouped, precision=lax.Precision.HIGHEST)
    head_cols = attended.shape[1]
    input_side = jnp.concatenate(
        [jnp.zeros((row_count, head_cols + branch_width), jnp.bfloat16), pre_grad], axis=1
    )
    grad_side = jnp.concatenate(
        [attended, branch_act, jnp.zeros((row_count, branch_width), jnp.bfloat16)], axis=1
    )
    terms = contract_rows(
        full_both.reshape(2 * row_count, model_width),
        jnp.concatenate([input_side, grad_side], axis=0),
    ).astype(jnp.bfloat16)
    merged = lax.psum_scatter(terms, "tm", scatter_dimension=0, tiled=True).astype(jnp.float32)
    table_blocks = lax.all_to_all(
        table_term.astype(jnp.bfloat16).reshape(tm_count, -1, branch_width), "tm", 0, 0, tiled=True
    )
    summed = (
        merged[:, :head_cols].T,
        merged[:, head_cols + branch_width :],
        merged[:, head_cols : head_cols + branch_width].T,
        jnp.sum(table_blocks.astype(jnp.float32), axis=0),
    )
    input_term = contract_cols(pre_grad, branch_in)
    input_sum = sum_over_groups(input_term.astype(jnp.bfloat16), steps_here, tokens_here)
    input_grad = (out_grad.astype(jnp.float32) + input_sum).astype(jnp.bfloat16)
    weight_grads = (summed, input_grad)
    grad_heads = attended_grad.reshape(steps_here, tokens_here, heads_here, HD)
    value_all = jnp.einsum(
        "shqk,sqhe->skhe", probs_low, grad_heads, preferred_element_type=jnp.float32
    )
    prob_grad = jnp.einsum(
        "sqhe,skhe->shqk", grad_heads, value_heads, preferred_element_type=jnp.float32
    )
    centre = jnp.sum(prob_grad * probs, axis=-1, keepdims=True)
    score_grad = (probs * (prob_grad - centre) * score_scale).astype(jnp.bfloat16)
    query_grad = (
        jnp.einsum("shqk,skhe->sqhe", score_grad, key_heads, preferred_element_type=jnp.float32)
        .astype(jnp.bfloat16)
        .reshape(1, steps_here, tokens_here, head_width)
    )
    key_all = jnp.einsum(
        "shqk,sqhe->skhe", score_grad, query_heads, preferred_element_type=jnp.float32
    ).reshape(steps_here, 3 * tokens_here, head_width)
    value_all = value_all.reshape(steps_here, 3 * tokens_here, head_width)
    own_key = key_all[:, 2 * tokens_here :].astype(jnp.bfloat16)[None]
    own_value = value_all[:, 2 * tokens_here :].astype(jnp.bfloat16)[None]
    toward_far = jnp.stack(
        [jnp.sum(key_all[:, :tokens_here], axis=0), jnp.sum(value_all[:, :tokens_here], axis=0)]
    )
    toward_near = jnp.stack(
        [
            jnp.sum(key_all[:, tokens_here : 2 * tokens_here], axis=0),
            jnp.sum(value_all[:, tokens_here : 2 * tokens_here], axis=0),
        ]
    )
    from_next = from_behind(toward_near.astype(jnp.bfloat16), "tm", -1).astype(toward_near.dtype)
    from_after = from_behind(toward_far.astype(jnp.bfloat16), "tm", -2).astype(toward_far.dtype)
    received = from_next + from_after
    attention_grads = (query_grad, own_key, own_value, received[None])
    summed, input_grad = weight_grads
    query_grad, own_key, own_value, cache_grad = attention_grads
    return (
        layer_out,
        input_grad,
        query_grad,
        own_key,
        own_value,
        cache_grad,
        summed[0],
        summed[1],
        summed[2],
        summed[3],
    )


def solution(mesh):
    in_specs = (
        P("tm", None, None, "tensor"),
        P("tm", None, None, "tensor"),
        P("tm", None, None, "tensor"),
        P("tm", None, None, "tensor"),
        P("tm", None, None, "tensor"),
        P("tensor", None),
        P(None, "tensor"),
        P("tensor", None),
        P(None, "tensor"),
        P("tm", None),
        P("tm"),
        P("tm", None, None, "tensor"),
    )
    out_specs = (
        P("tm", None, None, "tensor"),
        P("tm", None, None, "tensor"),
        P("tm", None, None, "tensor"),
        P("tm", None, None, "tensor"),
        P("tm", None, None, "tensor"),
        P("tm", None, None, "tensor"),
        P("tensor", "tm"),
        P("tm", "tensor"),
        P("tensor", "tm"),
        P("tm", "tensor"),
    )
    return jax.shard_map(body, mesh=mesh, in_specs=in_specs, out_specs=out_specs, check_vma=False)
```

```python
import jax
import jax.numpy as jnp
from jax import lax
from jax.sharding import PartitionSpec as P

HD = 128


GELU_C = 0.7978845608028654
GELU_A = 0.044715


def from_behind(value, axis, steps):
    count = lax.axis_size(axis)
    first, last = (max(0, -steps), min(count, count - steps))
    return lax.ppermute(value, axis, [(source, source + steps) for source in range(first, last)])


def gelu_value(inputs):
    inner = GELU_C * (inputs + GELU_A * inputs * inputs * inputs)
    return 0.5 * inputs * (1.0 + jnp.tanh(inner))


def gelu_slope(inputs):
    tangent = jnp.tanh(GELU_C * (inputs + GELU_A * inputs * inputs * inputs))
    return 0.5 * (1.0 + tangent) + 0.5 * inputs * (1.0 - tangent * tangent) * GELU_C * (
        1.0 + 3.0 * GELU_A * inputs * inputs
    )


def contract_rows(left, right):
    return lax.dot_general(
        left, right, (((0,), (0,)), ((), ())), preferred_element_type=jnp.float32
    )


def contract_cols(left, right):
    return lax.dot_general(
        left, right, (((1,), (1,)), ((), ())), preferred_element_type=jnp.float32
    )


TM = ("tmo", "core")


def two_stage_scatter(terms):
    outer = lax.axis_size("tmo")
    pairs = lax.axis_size("core")
    side = lax.axis_index("core")
    rows, width = terms.shape
    split = terms.reshape(outer, pairs, rows // (outer * pairs), width)
    given = lax.dynamic_index_in_dim(split, pairs - 1 - side, axis=1, keepdims=False)
    kept = lax.dynamic_index_in_dim(split, side, axis=1, keepdims=False)
    got = lax.ppermute(given, "core", [(0, 1), (1, 0)])
    paired = (kept.astype(jnp.float32) + got.astype(jnp.float32)).astype(jnp.bfloat16)
    return lax.psum_scatter(paired, "tmo", scatter_dimension=0, tiled=True)[0]


def sum_over_groups(partial, steps_here, tokens_here):
    count = lax.axis_size("tensor")
    rows, width = partial.shape
    blocks = partial.reshape(rows, count, width // count)
    received = lax.all_to_all(blocks, "tensor", 1, 1, tiled=True)
    total = jnp.sum(received.astype(jnp.float32), axis=1)
    return total.reshape(1, steps_here, tokens_here, width // count)


def body(
    hidden_in,
    noisy_queries,
    noisy_keys,
    noisy_values,
    clean_cache,
    out_proj,
    branch_in,
    branch_out,
    action_table,
    actions,
    offsets,
    out_grad,
):
    steps_here = noisy_queries.shape[1]
    tokens_here = noisy_queries.shape[2]
    head_width = noisy_queries.shape[3]
    heads_here = head_width // HD
    model_width = out_proj.shape[1]
    row_count = steps_here * tokens_here
    action_count = actions.shape[1]
    score_scale = HD ** (-0.5)
    full_both = lax.all_gather(
        jnp.concatenate([hidden_in, out_grad], axis=0), "tensor", axis=3, tiled=True
    )
    input_rows = full_both[0].reshape(row_count, model_width)
    grad_rows = full_both[1].reshape(row_count, model_width)
    own_cache = clean_cache[0]
    nearer = from_behind(own_cache, TM, 1)
    farther = from_behind(own_cache, TM, 2)
    reach = offsets[0]
    allowed = jnp.concatenate(
        [
            jnp.full((tokens_here,), reach >= 2),
            jnp.full((tokens_here,), reach >= 1),
            jnp.ones((tokens_here,), bool),
        ]
    )
    block_shape = (steps_here, tokens_here, head_width)
    key_block = jnp.concatenate(
        [
            jnp.broadcast_to(farther[0], block_shape),
            jnp.broadcast_to(nearer[0], block_shape),
            noisy_keys[0],
        ],
        axis=1,
    )
    value_block = jnp.concatenate(
        [
            jnp.broadcast_to(farther[1], block_shape),
            jnp.broadcast_to(nearer[1], block_shape),
            noisy_values[0],
        ],
        axis=1,
    )
    query_heads = noisy_queries[0].reshape(steps_here, tokens_here, heads_here, HD)
    key_heads = key_block.reshape(steps_here, 3 * tokens_here, heads_here, HD)
    value_heads = value_block.reshape(steps_here, 3 * tokens_here, heads_here, HD)
    scores = (
        jnp.einsum("sqhe,skhe->shqk", query_heads, key_heads, preferred_element_type=jnp.float32)
        * score_scale
    )
    masked = jnp.where(allowed[None, None, None, :], scores, -1e30)
    largest = jnp.max(masked, axis=-1, keepdims=True)
    raised = jnp.exp(masked - largest)
    probs = raised / jnp.sum(raised, axis=-1, keepdims=True)
    probs_low = probs.astype(jnp.bfloat16)
    attended = (
        jnp.einsum("shqk,skhe->sqhe", probs_low, value_heads, preferred_element_type=jnp.float32)
        .astype(jnp.bfloat16)
        .reshape(row_count, head_width)
    )
    onehot = (actions[0][:, None] == jnp.arange(action_table.shape[0])[None, :]).astype(
        jnp.bfloat16
    )
    action_rows = jnp.dot(onehot, action_table, preferred_element_type=jnp.float32)
    branch_width = branch_in.shape[1]
    pre_act = (
        jnp.dot(input_rows, branch_in, preferred_element_type=jnp.float32).reshape(
            steps_here, action_count, tokens_here // action_count, branch_width
        )
        + action_rows[None, :, None, :]
    )
    pre_act = pre_act.reshape(row_count, branch_width)
    branch_act = gelu_value(pre_act).astype(jnp.bfloat16)
    partial_value = jnp.dot(attended, out_proj, preferred_element_type=jnp.float32) + jnp.dot(
        branch_act, branch_out, preferred_element_type=jnp.float32
    )
    layer_sum = sum_over_groups(partial_value.astype(jnp.bfloat16), steps_here, tokens_here)
    layer_out = (hidden_in.astype(jnp.float32) + layer_sum).astype(jnp.bfloat16)
    attended_grad = contract_cols(grad_rows, out_proj).astype(jnp.bfloat16)
    pre_grad = (contract_cols(grad_rows, branch_out) * gelu_slope(pre_act)).astype(jnp.bfloat16)
    tm_count = lax.axis_size(TM)
    grouped = jnp.sum(
        pre_grad.reshape(
            steps_here, action_count, tokens_here // action_count, branch_width
        ).astype(jnp.float32),
        axis=(0, 2),
    )
    table_term = jnp.dot(onehot.astype(jnp.float32).T, grouped, precision=lax.Precision.HIGHEST)
    head_cols = attended.shape[1]
    input_side = jnp.concatenate(
        [jnp.zeros((row_count, head_cols + branch_width), jnp.bfloat16), pre_grad], axis=1
    )
    grad_side = jnp.concatenate(
        [attended, branch_act, jnp.zeros((row_count, branch_width), jnp.bfloat16)], axis=1
    )
    terms = contract_rows(
        full_both.reshape(2 * row_count, model_width),
        jnp.concatenate([input_side, grad_side], axis=0),
    ).astype(jnp.bfloat16)
    merged = two_stage_scatter(terms).astype(jnp.float32)
    table_blocks = lax.all_to_all(
        table_term.astype(jnp.bfloat16).reshape(tm_count, -1, branch_width), TM, 0, 0, tiled=True
    )
    summed = (
        merged[:, :head_cols].T,
        merged[:, head_cols + branch_width :],
        merged[:, head_cols : head_cols + branch_width].T,
        jnp.sum(table_blocks.astype(jnp.float32), axis=0),
    )
    input_term = contract_cols(pre_grad, branch_in)
    input_sum = sum_over_groups(input_term.astype(jnp.bfloat16), steps_here, tokens_here)
    input_grad = (out_grad.astype(jnp.float32) + input_sum).astype(jnp.bfloat16)
    weight_grads = (summed, input_grad)
    grad_heads = attended_grad.reshape(steps_here, tokens_here, heads_here, HD)
    value_all = jnp.einsum(
        "shqk,sqhe->skhe", probs_low, grad_heads, preferred_element_type=jnp.float32
    )
    prob_grad = jnp.einsum(
        "sqhe,skhe->shqk", grad_heads, value_heads, preferred_element_type=jnp.float32
    )
    centre = jnp.sum(prob_grad * probs, axis=-1, keepdims=True)
    score_grad = (probs * (prob_grad - centre) * score_scale).astype(jnp.bfloat16)
    query_grad = (
        jnp.einsum("shqk,skhe->sqhe", score_grad, key_heads, preferred_element_type=jnp.float32)
        .astype(jnp.bfloat16)
        .reshape(1, steps_here, tokens_here, head_width)
    )
    key_all = jnp.einsum(
        "shqk,sqhe->skhe", score_grad, query_heads, preferred_element_type=jnp.float32
    ).reshape(steps_here, 3 * tokens_here, head_width)
    value_all = value_all.reshape(steps_here, 3 * tokens_here, head_width)
    own_key = key_all[:, 2 * tokens_here :].astype(jnp.bfloat16)[None]
    own_value = value_all[:, 2 * tokens_here :].astype(jnp.bfloat16)[None]
    toward_far = jnp.stack(
        [jnp.sum(key_all[:, :tokens_here], axis=0), jnp.sum(value_all[:, :tokens_here], axis=0)]
    )
    toward_near = jnp.stack(
        [
            jnp.sum(key_all[:, tokens_here : 2 * tokens_here], axis=0),
            jnp.sum(value_all[:, tokens_here : 2 * tokens_here], axis=0),
        ]
    )
    from_next = from_behind(toward_near.astype(jnp.bfloat16), TM, -1).astype(toward_near.dtype)
    from_after = from_behind(toward_far.astype(jnp.bfloat16), TM, -2).astype(toward_far.dtype)
    received = from_next + from_after
    attention_grads = (query_grad, own_key, own_value, received[None])
    summed, input_grad = weight_grads
    query_grad, own_key, own_value, cache_grad = attention_grads
    return (
        layer_out,
        input_grad,
        query_grad,
        own_key,
        own_value,
        cache_grad,
        summed[0],
        summed[1],
        summed[2],
        summed[3],
    )


def solution(mesh):
    in_specs = (
        P("tm", None, None, "tensor"),
        P("tm", None, None, "tensor"),
        P("tm", None, None, "tensor"),
        P("tm", None, None, "tensor"),
        P("tm", None, None, "tensor"),
        P("tensor", None),
        P(None, "tensor"),
        P("tensor", None),
        P(None, "tensor"),
        P("tm", None),
        P("tm"),
        P("tm", None, None, "tensor"),
    )
    out_specs = (
        P("tm", None, None, "tensor"),
        P("tm", None, None, "tensor"),
        P("tm", None, None, "tensor"),
        P("tm", None, None, "tensor"),
        P("tm", None, None, "tensor"),
        P("tm", None, None, "tensor"),
        P("tensor", "tm"),
        P("tm", "tensor"),
        P("tensor", "tm"),
        P("tm", "tensor"),
    )
    shape = mesh.devices.shape
    inner = jax.sharding.Mesh(
        mesh.devices.reshape(shape[0] // 2, 2, shape[1]), ("tmo", "core", "tensor")
    )
    swap = lambda spec: P(*[TM if part == "tm" else part for part in spec])
    return jax.shard_map(
        body,
        mesh=inner,
        in_specs=tuple(swap(s) for s in in_specs),
        out_specs=tuple(swap(s) for s in out_specs),
        check_vma=False,
    )
```

```python
import jax
import jax.numpy as jnp
from jax import lax
from jax.sharding import PartitionSpec as P

HD = 128


GELU_C = 0.7978845608028654
GELU_A = 0.044715


def from_behind(value, axis, steps):
    count = lax.axis_size(axis)
    first, last = (max(0, -steps), min(count, count - steps))
    return lax.ppermute(value, axis, [(source, source + steps) for source in range(first, last)])


def gelu_value(inputs):
    inner = GELU_C * (inputs + GELU_A * inputs * inputs * inputs)
    return 0.5 * inputs * (1.0 + jnp.tanh(inner))


def gelu_slope(inputs):
    tangent = jnp.tanh(GELU_C * (inputs + GELU_A * inputs * inputs * inputs))
    return 0.5 * (1.0 + tangent) + 0.5 * inputs * (1.0 - tangent * tangent) * GELU_C * (
        1.0 + 3.0 * GELU_A * inputs * inputs
    )


def contract_rows(left, right):
    return lax.dot_general(
        left, right, (((0,), (0,)), ((), ())), preferred_element_type=jnp.float32
    )


def contract_cols(left, right):
    return lax.dot_general(
        left, right, (((1,), (1,)), ((), ())), preferred_element_type=jnp.float32
    )


TM = ("tmo", "core")


def two_stage_scatter(terms):
    outer = lax.axis_size("tmo")
    pairs = lax.axis_size("core")
    side = lax.axis_index("core")
    rows, width = terms.shape
    split = terms.reshape(outer, pairs, rows // (outer * pairs), width)
    given = lax.dynamic_index_in_dim(split, pairs - 1 - side, axis=1, keepdims=False)
    kept = lax.dynamic_index_in_dim(split, side, axis=1, keepdims=False)
    got = lax.ppermute(given, "core", [(0, 1), (1, 0)])
    paired = (kept.astype(jnp.float32) + got.astype(jnp.float32)).astype(jnp.bfloat16)
    return lax.psum_scatter(paired, "tmo", scatter_dimension=0, tiled=True)[0]


def sum_over_groups(partial, steps_here, tokens_here):
    count = lax.axis_size("tensor")
    rows, width = partial.shape
    blocks = partial.reshape(rows, count, width // count)
    received = lax.all_to_all(blocks, "tensor", 1, 1, tiled=True)
    total = jnp.sum(received.astype(jnp.float32), axis=1)
    return total.reshape(1, steps_here, tokens_here, width // count)


def body(
    hidden_in,
    noisy_queries,
    noisy_keys,
    noisy_values,
    clean_cache,
    out_proj,
    branch_in,
    branch_out,
    action_table,
    actions,
    offsets,
    out_grad,
):
    steps_here = noisy_queries.shape[1]
    tokens_here = noisy_queries.shape[2]
    head_width = noisy_queries.shape[3]
    heads_here = head_width // HD
    model_width = out_proj.shape[1]
    row_count = steps_here * tokens_here
    action_count = actions.shape[1]
    score_scale = HD ** (-0.5)
    own_cache = clean_cache[0]
    nearer = from_behind(own_cache, TM, 1)
    farther = from_behind(own_cache, TM, 2)
    reach = offsets[0]
    allowed = jnp.concatenate(
        [
            jnp.full((tokens_here,), reach >= 2),
            jnp.full((tokens_here,), reach >= 1),
            jnp.ones((tokens_here,), bool),
        ]
    )
    block_shape = (steps_here, tokens_here, head_width)
    key_block = jnp.concatenate(
        [
            jnp.broadcast_to(farther[0], block_shape),
            jnp.broadcast_to(nearer[0], block_shape),
            noisy_keys[0],
        ],
        axis=1,
    )
    value_block = jnp.concatenate(
        [
            jnp.broadcast_to(farther[1], block_shape),
            jnp.broadcast_to(nearer[1], block_shape),
            noisy_values[0],
        ],
        axis=1,
    )
    query_heads = noisy_queries[0].reshape(steps_here, tokens_here, heads_here, HD)
    key_heads = key_block.reshape(steps_here, 3 * tokens_here, heads_here, HD)
    value_heads = value_block.reshape(steps_here, 3 * tokens_here, heads_here, HD)
    scores = (
        jnp.einsum("sqhe,skhe->shqk", query_heads, key_heads, preferred_element_type=jnp.float32)
        * score_scale
    )
    masked = jnp.where(allowed[None, None, None, :], scores, -1e30)
    largest = jnp.max(masked, axis=-1, keepdims=True)
    raised = jnp.exp(masked - largest)
    probs = raised / jnp.sum(raised, axis=-1, keepdims=True)
    probs_low = probs.astype(jnp.bfloat16)
    attended = (
        jnp.einsum("shqk,skhe->sqhe", probs_low, value_heads, preferred_element_type=jnp.float32)
        .astype(jnp.bfloat16)
        .reshape(steps_here, tokens_here, head_width)
    )
    onehot = (actions[0][:, None] == jnp.arange(action_table.shape[0])[None, :]).astype(
        jnp.bfloat16
    )
    action_rows = jnp.dot(onehot, action_table, preferred_element_type=jnp.float32)
    branch_width = branch_in.shape[1]
    run_length = tokens_here // action_count
    tm_count = lax.axis_size(TM)
    partials, input_terms, terms, grouped = [], [], None, None
    query_parts, own_keys, own_values, far_parts, near_parts = [], [], [], [], []
    gathered = [
        lax.all_gather(
            jnp.stack([hidden_in[0, step], out_grad[0, step]]), "tensor", axis=2, tiled=True
        )
        for step in range(steps_here)
    ]
    for step in range(steps_here):
        both = gathered[step]
        pre_act = (
            jnp.dot(both[0], branch_in, preferred_element_type=jnp.float32).reshape(
                action_count, run_length, branch_width
            )
            + action_rows[:, None, :]
        ).reshape(tokens_here, branch_width)
        branch_act = gelu_value(pre_act).astype(jnp.bfloat16)
        attended_here = attended[step]
        partials.append(
            jnp.dot(attended_here, out_proj, preferred_element_type=jnp.float32)
            + jnp.dot(branch_act, branch_out, preferred_element_type=jnp.float32)
        )
        attended_grad = contract_cols(both[1], out_proj).astype(jnp.bfloat16)
        pre_grad = (contract_cols(both[1], branch_out) * gelu_slope(pre_act)).astype(
            jnp.bfloat16
        )
        input_terms.append(contract_cols(pre_grad, branch_in))
        head_cols = attended_here.shape[1]
        input_side = jnp.concatenate(
            [jnp.zeros((tokens_here, head_cols + branch_width), jnp.bfloat16), pre_grad], axis=1
        )
        grad_side = jnp.concatenate(
            [attended_here, branch_act, jnp.zeros((tokens_here, branch_width), jnp.bfloat16)],
            axis=1,
        )
        term = contract_rows(
            both.reshape(2 * tokens_here, model_width),
            jnp.concatenate([input_side, grad_side], axis=0),
        )
        terms = term if terms is None else terms + term
        runs = jnp.sum(
            pre_grad.reshape(action_count, run_length, branch_width).astype(jnp.float32), axis=1
        )
        grouped = runs if grouped is None else grouped + runs
        window = slice(step, step + 1)
        grad_heads = attended_grad.reshape(1, tokens_here, heads_here, HD)
        value_all = jnp.einsum(
            "shqk,sqhe->skhe", probs_low[window], grad_heads, preferred_element_type=jnp.float32
        )
        prob_grad = jnp.einsum(
            "sqhe,skhe->shqk", grad_heads, value_heads[window], preferred_element_type=jnp.float32
        )
        centre = jnp.sum(prob_grad * probs[window], axis=-1, keepdims=True)
        score_grad = (probs[window] * (prob_grad - centre) * score_scale).astype(jnp.bfloat16)
        query_parts.append(
            jnp.einsum(
                "shqk,skhe->sqhe", score_grad, key_heads[window], preferred_element_type=jnp.float32
            )
            .astype(jnp.bfloat16)
            .reshape(1, tokens_here, head_width)
        )
        key_all = jnp.einsum(
            "shqk,sqhe->skhe", score_grad, query_heads[window], preferred_element_type=jnp.float32
        ).reshape(3 * tokens_here, head_width)
        value_all = value_all.reshape(3 * tokens_here, head_width)
        own_keys.append(key_all[2 * tokens_here :].astype(jnp.bfloat16))
        own_values.append(value_all[2 * tokens_here :].astype(jnp.bfloat16))
        far_parts.append(jnp.stack([key_all[:tokens_here], value_all[:tokens_here]]))
        near_parts.append(
            jnp.stack(
                [key_all[tokens_here : 2 * tokens_here], value_all[tokens_here : 2 * tokens_here]]
            )
        )
        if step + 1 < steps_here:
            carried = (partials, input_terms, terms, grouped, query_parts, own_keys, own_values)
            gathered[step + 1], carried, far_parts, near_parts = lax.optimization_barrier(
                (gathered[step + 1], carried, far_parts, near_parts)
            )
            partials, input_terms, terms, grouped, query_parts, own_keys, own_values = carried
    layer_sum = sum_over_groups(
        jnp.concatenate(partials, axis=0).astype(jnp.bfloat16), steps_here, tokens_here
    )
    layer_out = (hidden_in.astype(jnp.float32) + layer_sum).astype(jnp.bfloat16)
    table_term = jnp.dot(onehot.astype(jnp.float32).T, grouped, precision=lax.Precision.HIGHEST)
    merged = two_stage_scatter(terms.astype(jnp.bfloat16)).astype(jnp.float32)
    table_blocks = lax.all_to_all(
        table_term.astype(jnp.bfloat16).reshape(tm_count, -1, branch_width), TM, 0, 0, tiled=True
    )
    summed = (
        merged[:, :head_cols].T,
        merged[:, head_cols + branch_width :],
        merged[:, head_cols : head_cols + branch_width].T,
        jnp.sum(table_blocks.astype(jnp.float32), axis=0),
    )
    input_sum = sum_over_groups(
        jnp.concatenate(input_terms, axis=0).astype(jnp.bfloat16), steps_here, tokens_here
    )
    input_grad = (out_grad.astype(jnp.float32) + input_sum).astype(jnp.bfloat16)
    query_grad = jnp.concatenate(query_parts, axis=0)[None]
    own_key = jnp.stack(own_keys)[None]
    own_value = jnp.stack(own_values)[None]
    toward_far = sum(far_parts)
    toward_near = sum(near_parts)
    from_next = from_behind(toward_near.astype(jnp.bfloat16), TM, -1).astype(toward_near.dtype)
    from_after = from_behind(toward_far.astype(jnp.bfloat16), TM, -2).astype(toward_far.dtype)
    cache_grad = (from_next + from_after)[None]
    return (
        layer_out,
        input_grad,
        query_grad,
        own_key,
        own_value,
        cache_grad,
        summed[0],
        summed[1],
        summed[2],
        summed[3],
    )


def solution(mesh):
    in_specs = (
        P("tm", None, None, "tensor"),
        P("tm", None, None, "tensor"),
        P("tm", None, None, "tensor"),
        P("tm", None, None, "tensor"),
        P("tm", None, None, "tensor"),
        P("tensor", None),
        P(None, "tensor"),
        P("tensor", None),
        P(None, "tensor"),
        P("tm", None),
        P("tm"),
        P("tm", None, None, "tensor"),
    )
    out_specs = (
        P("tm", None, None, "tensor"),
        P("tm", None, None, "tensor"),
        P("tm", None, None, "tensor"),
        P("tm", None, None, "tensor"),
        P("tm", None, None, "tensor"),
        P("tm", None, None, "tensor"),
        P("tensor", "tm"),
        P("tm", "tensor"),
        P("tensor", "tm"),
        P("tm", "tensor"),
    )
    shape = mesh.devices.shape
    inner = jax.sharding.Mesh(
        mesh.devices.reshape(shape[0] // 2, 2, shape[1]), ("tmo", "core", "tensor")
    )
    swap = lambda spec: P(*[TM if part == "tm" else part for part in spec])
    return jax.shard_map(
        body,
        mesh=inner,
        in_specs=tuple(swap(s) for s in in_specs),
        out_specs=tuple(swap(s) for s in out_specs),
        check_vma=False,
    )
```

```python
import jax
import jax.numpy as jnp
from jax import lax
from jax.sharding import PartitionSpec as P

HD = 128


GELU_C = 0.7978845608028654
GELU_A = 0.044715


def from_behind(value, axis, steps):
    count = lax.axis_size(axis)
    first, last = (max(0, -steps), min(count, count - steps))
    return lax.ppermute(value, axis, [(source, source + steps) for source in range(first, last)])


def gelu_value(inputs):
    inner = GELU_C * (inputs + GELU_A * inputs * inputs * inputs)
    return 0.5 * inputs * (1.0 + jnp.tanh(inner))


def gelu_slope(inputs):
    tangent = jnp.tanh(GELU_C * (inputs + GELU_A * inputs * inputs * inputs))
    return 0.5 * (1.0 + tangent) + 0.5 * inputs * (1.0 - tangent * tangent) * GELU_C * (
        1.0 + 3.0 * GELU_A * inputs * inputs
    )


def contract_rows(left, right):
    return lax.dot_general(
        left, right, (((0,), (0,)), ((), ())), preferred_element_type=jnp.float32
    )


def contract_cols(left, right):
    return lax.dot_general(
        left, right, (((1,), (1,)), ((), ())), preferred_element_type=jnp.float32
    )


TM = ("tmo", "core")


def two_stage_scatter(terms):
    outer = lax.axis_size("tmo")
    pairs = lax.axis_size("core")
    side = lax.axis_index("core")
    rows, width = terms.shape
    split = terms.reshape(outer, pairs, rows // (outer * pairs), width)
    given = lax.dynamic_index_in_dim(split, pairs - 1 - side, axis=1, keepdims=False)
    kept = lax.dynamic_index_in_dim(split, side, axis=1, keepdims=False)
    got = lax.ppermute(given, "core", [(0, 1), (1, 0)])
    paired = (kept.astype(jnp.float32) + got.astype(jnp.float32)).astype(jnp.bfloat16)
    return lax.psum_scatter(paired, "tmo", scatter_dimension=0, tiled=True)[0]


def sum_over_groups(partial, steps_here, tokens_here):
    rows, width = partial.shape
    return lax.psum_scatter(
        partial.reshape(1, steps_here, tokens_here, width),
        "tensor",
        scatter_dimension=3,
        tiled=True,
    ).astype(jnp.float32)


def body(
    hidden_in,
    noisy_queries,
    noisy_keys,
    noisy_values,
    clean_cache,
    out_proj,
    branch_in,
    branch_out,
    action_table,
    actions,
    offsets,
    out_grad,
):
    steps_here = noisy_queries.shape[1]
    tokens_here = noisy_queries.shape[2]
    head_width = noisy_queries.shape[3]
    heads_here = head_width // HD
    model_width = out_proj.shape[1]
    row_count = steps_here * tokens_here
    action_count = actions.shape[1]
    score_scale = HD ** (-0.5)
    full_both = lax.all_gather(
        jnp.concatenate([hidden_in, out_grad], axis=0), "tensor", axis=3, tiled=True
    )
    input_rows = full_both[0].reshape(row_count, model_width)
    grad_rows = full_both[1].reshape(row_count, model_width)
    own_cache = clean_cache[0]
    nearer = from_behind(own_cache, TM, 1)
    farther = from_behind(own_cache, TM, 2)
    reach = offsets[0]
    allowed = jnp.concatenate(
        [
            jnp.full((tokens_here,), reach >= 2),
            jnp.full((tokens_here,), reach >= 1),
            jnp.ones((tokens_here,), bool),
        ]
    )
    block_shape = (steps_here, tokens_here, head_width)
    key_block = jnp.concatenate(
        [
            jnp.broadcast_to(farther[0], block_shape),
            jnp.broadcast_to(nearer[0], block_shape),
            noisy_keys[0],
        ],
        axis=1,
    )
    value_block = jnp.concatenate(
        [
            jnp.broadcast_to(farther[1], block_shape),
            jnp.broadcast_to(nearer[1], block_shape),
            noisy_values[0],
        ],
        axis=1,
    )
    query_heads = noisy_queries[0].reshape(steps_here, tokens_here, heads_here, HD)
    key_heads = key_block.reshape(steps_here, 3 * tokens_here, heads_here, HD)
    value_heads = value_block.reshape(steps_here, 3 * tokens_here, heads_here, HD)
    scores = (
        jnp.einsum("sqhe,skhe->shqk", query_heads, key_heads, preferred_element_type=jnp.float32)
        * score_scale
    )
    masked = jnp.where(allowed[None, None, None, :], scores, -1e30)
    largest = jnp.max(masked, axis=-1, keepdims=True)
    raised = jnp.exp(masked - largest)
    probs = raised / jnp.sum(raised, axis=-1, keepdims=True)
    probs_low = probs.astype(jnp.bfloat16)
    attended = (
        jnp.einsum("shqk,skhe->sqhe", probs_low, value_heads, preferred_element_type=jnp.float32)
        .astype(jnp.bfloat16)
        .reshape(row_count, head_width)
    )
    onehot = (actions[0][:, None] == jnp.arange(action_table.shape[0])[None, :]).astype(
        jnp.bfloat16
    )
    action_rows = jnp.dot(onehot, action_table, preferred_element_type=jnp.float32)
    branch_width = branch_in.shape[1]
    pre_act = (
        jnp.dot(input_rows, branch_in, preferred_element_type=jnp.float32).reshape(
            steps_here, action_count, tokens_here // action_count, branch_width
        )
        + action_rows[None, :, None, :]
    )
    pre_act = pre_act.reshape(row_count, branch_width)
    branch_act = gelu_value(pre_act).astype(jnp.bfloat16)
    partial_value = jnp.dot(attended, out_proj, preferred_element_type=jnp.float32) + jnp.dot(
        branch_act, branch_out, preferred_element_type=jnp.float32
    )
    layer_sum = sum_over_groups(partial_value.astype(jnp.bfloat16), steps_here, tokens_here)
    layer_out = (hidden_in.astype(jnp.float32) + layer_sum).astype(jnp.bfloat16)
    attended_grad = contract_cols(grad_rows, out_proj).astype(jnp.bfloat16)
    pre_grad = (contract_cols(grad_rows, branch_out) * gelu_slope(pre_act)).astype(jnp.bfloat16)
    tm_count = lax.axis_size(TM)
    grouped = jnp.sum(
        pre_grad.reshape(
            steps_here, action_count, tokens_here // action_count, branch_width
        ).astype(jnp.float32),
        axis=(0, 2),
    )
    table_term = jnp.dot(onehot.astype(jnp.float32).T, grouped, precision=lax.Precision.HIGHEST)
    head_cols = attended.shape[1]
    input_side = jnp.concatenate(
        [jnp.zeros((row_count, head_cols + branch_width), jnp.bfloat16), pre_grad], axis=1
    )
    grad_side = jnp.concatenate(
        [attended, branch_act, jnp.zeros((row_count, branch_width), jnp.bfloat16)], axis=1
    )
    terms = contract_rows(
        full_both.reshape(2 * row_count, model_width),
        jnp.concatenate([input_side, grad_side], axis=0),
    ).astype(jnp.bfloat16)
    merged = two_stage_scatter(terms).astype(jnp.float32)
    table_blocks = lax.all_to_all(
        table_term.astype(jnp.bfloat16).reshape(tm_count, -1, branch_width), TM, 0, 0, tiled=True
    )
    summed = (
        merged[:, :head_cols].T,
        merged[:, head_cols + branch_width :],
        merged[:, head_cols : head_cols + branch_width].T,
        jnp.sum(table_blocks.astype(jnp.float32), axis=0),
    )
    input_term = contract_cols(pre_grad, branch_in)
    input_sum = sum_over_groups(input_term.astype(jnp.bfloat16), steps_here, tokens_here)
    input_grad = (out_grad.astype(jnp.float32) + input_sum).astype(jnp.bfloat16)
    weight_grads = (summed, input_grad)
    grad_heads = attended_grad.reshape(steps_here, tokens_here, heads_here, HD)
    value_all = jnp.einsum(
        "shqk,sqhe->skhe", probs_low, grad_heads, preferred_element_type=jnp.float32
    )
    prob_grad = jnp.einsum(
        "sqhe,skhe->shqk", grad_heads, value_heads, preferred_element_type=jnp.float32
    )
    centre = jnp.sum(prob_grad * probs, axis=-1, keepdims=True)
    score_grad = (probs * (prob_grad - centre) * score_scale).astype(jnp.bfloat16)
    query_grad = (
        jnp.einsum("shqk,skhe->sqhe", score_grad, key_heads, preferred_element_type=jnp.float32)
        .astype(jnp.bfloat16)
        .reshape(1, steps_here, tokens_here, head_width)
    )
    key_all = jnp.einsum(
        "shqk,sqhe->skhe", score_grad, query_heads, preferred_element_type=jnp.float32
    ).reshape(steps_here, 3 * tokens_here, head_width)
    value_all = value_all.reshape(steps_here, 3 * tokens_here, head_width)
    own_key = key_all[:, 2 * tokens_here :].astype(jnp.bfloat16)[None]
    own_value = value_all[:, 2 * tokens_here :].astype(jnp.bfloat16)[None]
    toward_far = jnp.stack(
        [jnp.sum(key_all[:, :tokens_here], axis=0), jnp.sum(value_all[:, :tokens_here], axis=0)]
    )
    toward_near = jnp.stack(
        [
            jnp.sum(key_all[:, tokens_here : 2 * tokens_here], axis=0),
            jnp.sum(value_all[:, tokens_here : 2 * tokens_here], axis=0),
        ]
    )
    from_next = from_behind(toward_near.astype(jnp.bfloat16), TM, -1).astype(toward_near.dtype)
    from_after = from_behind(toward_far.astype(jnp.bfloat16), TM, -2).astype(toward_far.dtype)
    received = from_next + from_after
    attention_grads = (query_grad, own_key, own_value, received[None])
    summed, input_grad = weight_grads
    query_grad, own_key, own_value, cache_grad = attention_grads
    return (
        layer_out,
        input_grad,
        query_grad,
        own_key,
        own_value,
        cache_grad,
        summed[0],
        summed[1],
        summed[2],
        summed[3],
    )


def solution(mesh):
    in_specs = (
        P("tm", None, None, "tensor"),
        P("tm", None, None, "tensor"),
        P("tm", None, None, "tensor"),
        P("tm", None, None, "tensor"),
        P("tm", None, None, "tensor"),
        P("tensor", None),
        P(None, "tensor"),
        P("tensor", None),
        P(None, "tensor"),
        P("tm", None),
        P("tm"),
        P("tm", None, None, "tensor"),
    )
    out_specs = (
        P("tm", None, None, "tensor"),
        P("tm", None, None, "tensor"),
        P("tm", None, None, "tensor"),
        P("tm", None, None, "tensor"),
        P("tm", None, None, "tensor"),
        P("tm", None, None, "tensor"),
        P("tensor", "tm"),
        P("tm", "tensor"),
        P("tensor", "tm"),
        P("tm", "tensor"),
    )
    shape = mesh.devices.shape
    inner = jax.sharding.Mesh(
        mesh.devices.reshape(shape[0] // 2, 2, shape[1]), ("tmo", "core", "tensor")
    )
    swap = lambda spec: P(*[TM if part == "tm" else part for part in spec])
    return jax.shard_map(
        body,
        mesh=inner,
        in_specs=tuple(swap(s) for s in in_specs),
        out_specs=tuple(swap(s) for s in out_specs),
        check_vma=False,
    )
```

```python
import jax
import jax.numpy as jnp
from jax import lax
from jax.sharding import PartitionSpec as P

HD = 128


GELU_C = 0.7978845608028654
GELU_A = 0.044715


def from_behind(value, axis, steps):
    count = lax.axis_size(axis)
    first, last = (max(0, -steps), min(count, count - steps))
    return lax.ppermute(value, axis, [(source, source + steps) for source in range(first, last)])


def gelu_value(inputs):
    inner = GELU_C * (inputs + GELU_A * inputs * inputs * inputs)
    return 0.5 * inputs * (1.0 + jnp.tanh(inner))


def gelu_slope(inputs):
    tangent = jnp.tanh(GELU_C * (inputs + GELU_A * inputs * inputs * inputs))
    return 0.5 * (1.0 + tangent) + 0.5 * inputs * (1.0 - tangent * tangent) * GELU_C * (
        1.0 + 3.0 * GELU_A * inputs * inputs
    )


def contract_rows(left, right):
    return lax.dot_general(
        left, right, (((0,), (0,)), ((), ())), preferred_element_type=jnp.float32
    )


def contract_cols(left, right):
    return lax.dot_general(
        left, right, (((1,), (1,)), ((), ())), preferred_element_type=jnp.float32
    )


TM = ("tmo", "core")


def two_stage_scatter(terms):
    outer = lax.axis_size("tmo")
    pairs = lax.axis_size("core")
    side = lax.axis_index("core")
    rows, width = terms.shape
    split = terms.reshape(outer, pairs, rows // (outer * pairs), width)
    given = lax.dynamic_index_in_dim(split, pairs - 1 - side, axis=1, keepdims=False)
    kept = lax.dynamic_index_in_dim(split, side, axis=1, keepdims=False)
    got = lax.ppermute(given, "core", [(0, 1), (1, 0)])
    paired = (kept.astype(jnp.float32) + got.astype(jnp.float32)).astype(jnp.bfloat16)
    return lax.psum_scatter(paired, "tmo", scatter_dimension=0, tiled=True)[0]


def sum_over_groups(partial, steps_here, tokens_here):
    count, rows, width = partial.shape
    return lax.psum_scatter(partial, "tensor", scatter_dimension=0, tiled=True).reshape(
        1, steps_here, tokens_here, width
    ).astype(jnp.float32)


def body(
    hidden_in,
    noisy_queries,
    noisy_keys,
    noisy_values,
    clean_cache,
    out_proj,
    branch_in,
    branch_out,
    action_table,
    actions,
    offsets,
    out_grad,
):
    steps_here = noisy_queries.shape[1]
    tokens_here = noisy_queries.shape[2]
    head_width = noisy_queries.shape[3]
    heads_here = head_width // HD
    model_width = out_proj.shape[1]
    row_count = steps_here * tokens_here
    action_count = actions.shape[1]
    score_scale = HD ** (-0.5)
    full_both = lax.all_gather(
        jnp.concatenate([hidden_in, out_grad], axis=0), "tensor", axis=3, tiled=True
    )
    input_rows = full_both[0].reshape(row_count, model_width)
    grad_rows = full_both[1].reshape(row_count, model_width)
    own_cache = clean_cache[0]
    nearer = from_behind(own_cache, TM, 1)
    farther = from_behind(own_cache, TM, 2)
    reach = offsets[0]
    allowed = jnp.concatenate(
        [
            jnp.full((tokens_here,), reach >= 2),
            jnp.full((tokens_here,), reach >= 1),
            jnp.ones((tokens_here,), bool),
        ]
    )
    block_shape = (steps_here, tokens_here, head_width)
    key_block = jnp.concatenate(
        [
            jnp.broadcast_to(farther[0], block_shape),
            jnp.broadcast_to(nearer[0], block_shape),
            noisy_keys[0],
        ],
        axis=1,
    )
    value_block = jnp.concatenate(
        [
            jnp.broadcast_to(farther[1], block_shape),
            jnp.broadcast_to(nearer[1], block_shape),
            noisy_values[0],
        ],
        axis=1,
    )
    query_heads = noisy_queries[0].reshape(steps_here, tokens_here, heads_here, HD)
    key_heads = key_block.reshape(steps_here, 3 * tokens_here, heads_here, HD)
    value_heads = value_block.reshape(steps_here, 3 * tokens_here, heads_here, HD)
    scores = (
        jnp.einsum("sqhe,skhe->shqk", query_heads, key_heads, preferred_element_type=jnp.float32)
        * score_scale
    )
    masked = jnp.where(allowed[None, None, None, :], scores, -1e30)
    largest = jnp.max(masked, axis=-1, keepdims=True)
    raised = jnp.exp(masked - largest)
    probs = raised / jnp.sum(raised, axis=-1, keepdims=True)
    probs_low = probs.astype(jnp.bfloat16)
    attended = (
        jnp.einsum("shqk,skhe->sqhe", probs_low, value_heads, preferred_element_type=jnp.float32)
        .astype(jnp.bfloat16)
        .reshape(row_count, head_width)
    )
    onehot = (actions[0][:, None] == jnp.arange(action_table.shape[0])[None, :]).astype(
        jnp.bfloat16
    )
    action_rows = jnp.dot(onehot, action_table, preferred_element_type=jnp.float32)
    branch_width = branch_in.shape[1]
    pre_act = (
        jnp.dot(input_rows, branch_in, preferred_element_type=jnp.float32).reshape(
            steps_here, action_count, tokens_here // action_count, branch_width
        )
        + action_rows[None, :, None, :]
    )
    pre_act = pre_act.reshape(row_count, branch_width)
    branch_act = gelu_value(pre_act).astype(jnp.bfloat16)
    group_count = lax.axis_size("tensor")
    group_width = model_width // group_count
    partial_value = jnp.einsum(
        "rk,kjn->jrn",
        attended,
        out_proj.reshape(-1, group_count, group_width),
        preferred_element_type=jnp.float32,
    ) + jnp.einsum(
        "rk,kjn->jrn",
        branch_act,
        branch_out.reshape(-1, group_count, group_width),
        preferred_element_type=jnp.float32,
    )
    layer_sum = sum_over_groups(partial_value.astype(jnp.bfloat16), steps_here, tokens_here)
    layer_out = (hidden_in.astype(jnp.float32) + layer_sum).astype(jnp.bfloat16)
    attended_grad = contract_cols(grad_rows, out_proj).astype(jnp.bfloat16)
    pre_grad = (contract_cols(grad_rows, branch_out) * gelu_slope(pre_act)).astype(jnp.bfloat16)
    tm_count = lax.axis_size(TM)
    grouped = jnp.sum(
        pre_grad.reshape(
            steps_here, action_count, tokens_here // action_count, branch_width
        ).astype(jnp.float32),
        axis=(0, 2),
    )
    table_term = jnp.dot(onehot.astype(jnp.float32).T, grouped, precision=lax.Precision.HIGHEST)
    head_cols = attended.shape[1]
    input_side = jnp.concatenate(
        [jnp.zeros((row_count, head_cols + branch_width), jnp.bfloat16), pre_grad], axis=1
    )
    grad_side = jnp.concatenate(
        [attended, branch_act, jnp.zeros((row_count, branch_width), jnp.bfloat16)], axis=1
    )
    terms = contract_rows(
        full_both.reshape(2 * row_count, model_width),
        jnp.concatenate([input_side, grad_side], axis=0),
    ).astype(jnp.bfloat16)
    merged = two_stage_scatter(terms).astype(jnp.float32)
    table_blocks = lax.all_to_all(
        table_term.astype(jnp.bfloat16).reshape(tm_count, -1, branch_width), TM, 0, 0, tiled=True
    )
    summed = (
        merged[:, :head_cols].T,
        merged[:, head_cols + branch_width :],
        merged[:, head_cols : head_cols + branch_width].T,
        jnp.sum(table_blocks.astype(jnp.float32), axis=0),
    )
    input_term = jnp.einsum(
        "rk,jnk->jrn",
        pre_grad,
        branch_in.reshape(group_count, group_width, -1),
        preferred_element_type=jnp.float32,
    )
    input_sum = sum_over_groups(input_term.astype(jnp.bfloat16), steps_here, tokens_here)
    input_grad = (out_grad.astype(jnp.float32) + input_sum).astype(jnp.bfloat16)
    weight_grads = (summed, input_grad)
    grad_heads = attended_grad.reshape(steps_here, tokens_here, heads_here, HD)
    value_all = jnp.einsum(
        "shqk,sqhe->skhe", probs_low, grad_heads, preferred_element_type=jnp.float32
    )
    prob_grad = jnp.einsum(
        "sqhe,skhe->shqk", grad_heads, value_heads, preferred_element_type=jnp.float32
    )
    centre = jnp.sum(prob_grad * probs, axis=-1, keepdims=True)
    score_grad = (probs * (prob_grad - centre) * score_scale).astype(jnp.bfloat16)
    query_grad = (
        jnp.einsum("shqk,skhe->sqhe", score_grad, key_heads, preferred_element_type=jnp.float32)
        .astype(jnp.bfloat16)
        .reshape(1, steps_here, tokens_here, head_width)
    )
    key_all = jnp.einsum(
        "shqk,sqhe->skhe", score_grad, query_heads, preferred_element_type=jnp.float32
    ).reshape(steps_here, 3 * tokens_here, head_width)
    value_all = value_all.reshape(steps_here, 3 * tokens_here, head_width)
    own_key = key_all[:, 2 * tokens_here :].astype(jnp.bfloat16)[None]
    own_value = value_all[:, 2 * tokens_here :].astype(jnp.bfloat16)[None]
    toward_far = jnp.stack(
        [jnp.sum(key_all[:, :tokens_here], axis=0), jnp.sum(value_all[:, :tokens_here], axis=0)]
    )
    toward_near = jnp.stack(
        [
            jnp.sum(key_all[:, tokens_here : 2 * tokens_here], axis=0),
            jnp.sum(value_all[:, tokens_here : 2 * tokens_here], axis=0),
        ]
    )
    from_next = from_behind(toward_near.astype(jnp.bfloat16), TM, -1).astype(toward_near.dtype)
    from_after = from_behind(toward_far.astype(jnp.bfloat16), TM, -2).astype(toward_far.dtype)
    received = from_next + from_after
    attention_grads = (query_grad, own_key, own_value, received[None])
    summed, input_grad = weight_grads
    query_grad, own_key, own_value, cache_grad = attention_grads
    return (
        layer_out,
        input_grad,
        query_grad,
        own_key,
        own_value,
        cache_grad,
        summed[0],
        summed[1],
        summed[2],
        summed[3],
    )


def solution(mesh):
    in_specs = (
        P("tm", None, None, "tensor"),
        P("tm", None, None, "tensor"),
        P("tm", None, None, "tensor"),
        P("tm", None, None, "tensor"),
        P("tm", None, None, "tensor"),
        P("tensor", None),
        P(None, "tensor"),
        P("tensor", None),
        P(None, "tensor"),
        P("tm", None),
        P("tm"),
        P("tm", None, None, "tensor"),
    )
    out_specs = (
        P("tm", None, None, "tensor"),
        P("tm", None, None, "tensor"),
        P("tm", None, None, "tensor"),
        P("tm", None, None, "tensor"),
        P("tm", None, None, "tensor"),
        P("tm", None, None, "tensor"),
        P("tensor", "tm"),
        P("tm", "tensor"),
        P("tensor", "tm"),
        P("tm", "tensor"),
    )
    shape = mesh.devices.shape
    inner = jax.sharding.Mesh(
        mesh.devices.reshape(shape[0] // 2, 2, shape[1]), ("tmo", "core", "tensor")
    )
    swap = lambda spec: P(*[TM if part == "tm" else part for part in spec])
    return jax.shard_map(
        body,
        mesh=inner,
        in_specs=tuple(swap(s) for s in in_specs),
        out_specs=tuple(swap(s) for s in out_specs),
        check_vma=False,
    )
```

```python
import jax
import jax.numpy as jnp
from jax import lax
from jax.sharding import PartitionSpec as P

HD = 128


GELU_C = 0.7978845608028654
GELU_A = 0.044715


def from_behind(value, axis, steps):
    count = lax.axis_size(axis)
    first, last = (max(0, -steps), min(count, count - steps))
    return lax.ppermute(value, axis, [(source, source + steps) for source in range(first, last)])


def gelu_value(inputs):
    inner = GELU_C * (inputs + GELU_A * inputs * inputs * inputs)
    return 0.5 * inputs * (1.0 + jnp.tanh(inner))


def gelu_slope(inputs):
    tangent = jnp.tanh(GELU_C * (inputs + GELU_A * inputs * inputs * inputs))
    return 0.5 * (1.0 + tangent) + 0.5 * inputs * (1.0 - tangent * tangent) * GELU_C * (
        1.0 + 3.0 * GELU_A * inputs * inputs
    )


def contract_rows(left, right):
    return lax.dot_general(
        left, right, (((0,), (0,)), ((), ())), preferred_element_type=jnp.float32
    )


def contract_cols(left, right):
    return lax.dot_general(
        left, right, (((1,), (1,)), ((), ())), preferred_element_type=jnp.float32
    )


TM = ("tmo", "core")


def two_stage_scatter(terms):
    outer = lax.axis_size("tmo")
    pairs = lax.axis_size("core")
    side = lax.axis_index("core")
    rows, width = terms.shape
    split = terms.reshape(outer, pairs, rows // (outer * pairs), width)
    given = lax.dynamic_index_in_dim(split, pairs - 1 - side, axis=1, keepdims=False)
    kept = lax.dynamic_index_in_dim(split, side, axis=1, keepdims=False)
    got = lax.ppermute(given, "core", [(0, 1), (1, 0)])
    paired = (kept.astype(jnp.float32) + got.astype(jnp.float32)).astype(jnp.bfloat16)
    return lax.psum_scatter(paired, "tmo", scatter_dimension=0, tiled=True)[0]


def sum_over_groups(partial, steps_here, tokens_here):
    count, rows, width = partial.shape
    return lax.psum_scatter(partial, "tensor", scatter_dimension=0, tiled=True).reshape(
        1, steps_here, tokens_here, width
    ).astype(jnp.float32)


def body(
    hidden_in,
    noisy_queries,
    noisy_keys,
    noisy_values,
    clean_cache,
    out_proj,
    branch_in,
    branch_out,
    action_table,
    actions,
    offsets,
    out_grad,
):
    steps_here = noisy_queries.shape[1]
    tokens_here = noisy_queries.shape[2]
    head_width = noisy_queries.shape[3]
    heads_here = head_width // HD
    model_width = out_proj.shape[1]
    row_count = steps_here * tokens_here
    action_count = actions.shape[1]
    score_scale = HD ** (-0.5)
    full_inputs = lax.all_gather(hidden_in, "tensor", axis=3, tiled=True)
    full_grads = lax.all_gather(out_grad, "tensor", axis=3, tiled=True)
    input_rows = full_inputs.reshape(row_count, model_width)
    grad_rows = full_grads.reshape(row_count, model_width)
    own_cache = clean_cache[0]
    nearer = from_behind(own_cache, TM, 1)
    farther = from_behind(own_cache, TM, 2)
    reach = offsets[0]
    allowed = jnp.concatenate(
        [
            jnp.full((tokens_here,), reach >= 2),
            jnp.full((tokens_here,), reach >= 1),
            jnp.ones((tokens_here,), bool),
        ]
    )
    block_shape = (steps_here, tokens_here, head_width)
    key_block = jnp.concatenate(
        [
            jnp.broadcast_to(farther[0], block_shape),
            jnp.broadcast_to(nearer[0], block_shape),
            noisy_keys[0],
        ],
        axis=1,
    )
    value_block = jnp.concatenate(
        [
            jnp.broadcast_to(farther[1], block_shape),
            jnp.broadcast_to(nearer[1], block_shape),
            noisy_values[0],
        ],
        axis=1,
    )
    query_heads = noisy_queries[0].reshape(steps_here, tokens_here, heads_here, HD)
    key_heads = key_block.reshape(steps_here, 3 * tokens_here, heads_here, HD)
    value_heads = value_block.reshape(steps_here, 3 * tokens_here, heads_here, HD)
    scores = (
        jnp.einsum("sqhe,skhe->shqk", query_heads, key_heads, preferred_element_type=jnp.float32)
        * score_scale
    )
    masked = jnp.where(allowed[None, None, None, :], scores, -1e30)
    largest = jnp.max(masked, axis=-1, keepdims=True)
    raised = jnp.exp(masked - largest)
    probs = raised / jnp.sum(raised, axis=-1, keepdims=True)
    probs_low = probs.astype(jnp.bfloat16)
    attended = (
        jnp.einsum("shqk,skhe->sqhe", probs_low, value_heads, preferred_element_type=jnp.float32)
        .astype(jnp.bfloat16)
        .reshape(row_count, head_width)
    )
    onehot = (actions[0][:, None] == jnp.arange(action_table.shape[0])[None, :]).astype(
        jnp.bfloat16
    )
    action_rows = jnp.dot(onehot, action_table, preferred_element_type=jnp.float32)
    branch_width = branch_in.shape[1]
    pre_act = (
        jnp.dot(input_rows, branch_in, preferred_element_type=jnp.float32).reshape(
            steps_here, action_count, tokens_here // action_count, branch_width
        )
        + action_rows[None, :, None, :]
    )
    pre_act = pre_act.reshape(row_count, branch_width)
    branch_act = gelu_value(pre_act).astype(jnp.bfloat16)
    group_count = lax.axis_size("tensor")
    group_width = model_width // group_count
    partial_value = jnp.einsum(
        "rk,kjn->jrn",
        attended,
        out_proj.reshape(-1, group_count, group_width),
        preferred_element_type=jnp.float32,
    ) + jnp.einsum(
        "rk,kjn->jrn",
        branch_act,
        branch_out.reshape(-1, group_count, group_width),
        preferred_element_type=jnp.float32,
    )
    layer_sum = sum_over_groups(partial_value.astype(jnp.bfloat16), steps_here, tokens_here)
    layer_out = (hidden_in.astype(jnp.float32) + layer_sum).astype(jnp.bfloat16)
    attended_grad = contract_cols(grad_rows, out_proj).astype(jnp.bfloat16)
    pre_grad = (contract_cols(grad_rows, branch_out) * gelu_slope(pre_act)).astype(jnp.bfloat16)
    tm_count = lax.axis_size(TM)
    grouped = jnp.sum(
        pre_grad.reshape(
            steps_here, action_count, tokens_here // action_count, branch_width
        ).astype(jnp.float32),
        axis=(0, 2),
    )
    table_term = jnp.dot(onehot.astype(jnp.float32).T, grouped, precision=lax.Precision.HIGHEST)
    head_cols = attended.shape[1]
    input_side = jnp.concatenate(
        [jnp.zeros((row_count, head_cols + branch_width), jnp.bfloat16), pre_grad], axis=1
    )
    grad_side = jnp.concatenate(
        [attended, branch_act, jnp.zeros((row_count, branch_width), jnp.bfloat16)], axis=1
    )
    terms = contract_rows(
        jnp.concatenate([input_rows, grad_rows], axis=0),
        jnp.concatenate([input_side, grad_side], axis=0),
    ).astype(jnp.bfloat16)
    merged = two_stage_scatter(terms).astype(jnp.float32)
    table_blocks = lax.all_to_all(
        table_term.astype(jnp.bfloat16).reshape(tm_count, -1, branch_width), TM, 0, 0, tiled=True
    )
    summed = (
        merged[:, :head_cols].T,
        merged[:, head_cols + branch_width :],
        merged[:, head_cols : head_cols + branch_width].T,
        jnp.sum(table_blocks.astype(jnp.float32), axis=0),
    )
    input_term = jnp.einsum(
        "rk,jnk->jrn",
        pre_grad,
        branch_in.reshape(group_count, group_width, -1),
        preferred_element_type=jnp.float32,
    )
    input_sum = sum_over_groups(input_term.astype(jnp.bfloat16), steps_here, tokens_here)
    input_grad = (out_grad.astype(jnp.float32) + input_sum).astype(jnp.bfloat16)
    weight_grads = (summed, input_grad)
    grad_heads = attended_grad.reshape(steps_here, tokens_here, heads_here, HD)
    value_all = jnp.einsum(
        "shqk,sqhe->skhe", probs_low, grad_heads, preferred_element_type=jnp.float32
    )
    prob_grad = jnp.einsum(
        "sqhe,skhe->shqk", grad_heads, value_heads, preferred_element_type=jnp.float32
    )
    centre = jnp.sum(prob_grad * probs, axis=-1, keepdims=True)
    score_grad = (probs * (prob_grad - centre) * score_scale).astype(jnp.bfloat16)
    query_grad = (
        jnp.einsum("shqk,skhe->sqhe", score_grad, key_heads, preferred_element_type=jnp.float32)
        .astype(jnp.bfloat16)
        .reshape(1, steps_here, tokens_here, head_width)
    )
    key_all = jnp.einsum(
        "shqk,sqhe->skhe", score_grad, query_heads, preferred_element_type=jnp.float32
    ).reshape(steps_here, 3 * tokens_here, head_width)
    value_all = value_all.reshape(steps_here, 3 * tokens_here, head_width)
    own_key = key_all[:, 2 * tokens_here :].astype(jnp.bfloat16)[None]
    own_value = value_all[:, 2 * tokens_here :].astype(jnp.bfloat16)[None]
    toward_far = jnp.stack(
        [jnp.sum(key_all[:, :tokens_here], axis=0), jnp.sum(value_all[:, :tokens_here], axis=0)]
    )
    toward_near = jnp.stack(
        [
            jnp.sum(key_all[:, tokens_here : 2 * tokens_here], axis=0),
            jnp.sum(value_all[:, tokens_here : 2 * tokens_here], axis=0),
        ]
    )
    from_next = from_behind(toward_near.astype(jnp.bfloat16), TM, -1).astype(toward_near.dtype)
    from_after = from_behind(toward_far.astype(jnp.bfloat16), TM, -2).astype(toward_far.dtype)
    received = from_next + from_after
    attention_grads = (query_grad, own_key, own_value, received[None])
    summed, input_grad = weight_grads
    query_grad, own_key, own_value, cache_grad = attention_grads
    return (
        layer_out,
        input_grad,
        query_grad,
        own_key,
        own_value,
        cache_grad,
        summed[0],
        summed[1],
        summed[2],
        summed[3],
    )


def solution(mesh):
    in_specs = (
        P("tm", None, None, "tensor"),
        P("tm", None, None, "tensor"),
        P("tm", None, None, "tensor"),
        P("tm", None, None, "tensor"),
        P("tm", None, None, "tensor"),
        P("tensor", None),
        P(None, "tensor"),
        P("tensor", None),
        P(None, "tensor"),
        P("tm", None),
        P("tm"),
        P("tm", None, None, "tensor"),
    )
    out_specs = (
        P("tm", None, None, "tensor"),
        P("tm", None, None, "tensor"),
        P("tm", None, None, "tensor"),
        P("tm", None, None, "tensor"),
        P("tm", None, None, "tensor"),
        P("tm", None, None, "tensor"),
        P("tensor", "tm"),
        P("tm", "tensor"),
        P("tensor", "tm"),
        P("tm", "tensor"),
    )
    shape = mesh.devices.shape
    inner = jax.sharding.Mesh(
        mesh.devices.reshape(shape[0] // 2, 2, shape[1]), ("tmo", "core", "tensor")
    )
    swap = lambda spec: P(*[TM if part == "tm" else part for part in spec])
    return jax.shard_map(
        body,
        mesh=inner,
        in_specs=tuple(swap(s) for s in in_specs),
        out_specs=tuple(swap(s) for s in out_specs),
        check_vma=False,
    )
```

```python
import jax
import jax.numpy as jnp
from jax import lax
from jax.sharding import PartitionSpec as P

HD = 128


GELU_C = 0.7978845608028654
GELU_A = 0.044715


def from_behind(value, axis, steps):
    count = lax.axis_size(axis)
    first, last = (max(0, -steps), min(count, count - steps))
    return lax.ppermute(value, axis, [(source, source + steps) for source in range(first, last)])


def gelu_value(inputs):
    inner = GELU_C * (inputs + GELU_A * inputs * inputs * inputs)
    return 0.5 * inputs * (1.0 + jnp.tanh(inner))


def gelu_slope(inputs):
    tangent = jnp.tanh(GELU_C * (inputs + GELU_A * inputs * inputs * inputs))
    return 0.5 * (1.0 + tangent) + 0.5 * inputs * (1.0 - tangent * tangent) * GELU_C * (
        1.0 + 3.0 * GELU_A * inputs * inputs
    )


def contract_rows(left, right):
    return lax.dot_general(
        left, right, (((0,), (0,)), ((), ())), preferred_element_type=jnp.float32
    )


def contract_cols(left, right):
    return lax.dot_general(
        left, right, (((1,), (1,)), ((), ())), preferred_element_type=jnp.float32
    )


TM = ("tmo", "core")


def two_stage_scatter(terms):
    outer = lax.axis_size("tmo")
    pairs = lax.axis_size("core")
    side = lax.axis_index("core")
    rows, width = terms.shape
    split = terms.reshape(outer, pairs, rows // (outer * pairs), width)
    given = lax.dynamic_index_in_dim(split, pairs - 1 - side, axis=1, keepdims=False)
    kept = lax.dynamic_index_in_dim(split, side, axis=1, keepdims=False)
    got = lax.ppermute(given, "core", [(0, 1), (1, 0)])
    paired = (kept.astype(jnp.float32) + got.astype(jnp.float32)).astype(jnp.bfloat16)
    return lax.psum_scatter(paired, "tmo", scatter_dimension=0, tiled=True)[0]


def sum_over_groups(partial, steps_here, tokens_here):
    count, rows, width = partial.shape
    return lax.psum_scatter(partial, "tensor", scatter_dimension=0, tiled=True).reshape(
        1, steps_here, tokens_here, width
    ).astype(jnp.float32)


def body(
    hidden_in,
    noisy_queries,
    noisy_keys,
    noisy_values,
    clean_cache,
    out_proj,
    branch_in,
    branch_out,
    action_table,
    actions,
    offsets,
    out_grad,
):
    steps_here = noisy_queries.shape[1]
    tokens_here = noisy_queries.shape[2]
    head_width = noisy_queries.shape[3]
    heads_here = head_width // HD
    model_width = out_proj.shape[1]
    row_count = steps_here * tokens_here
    action_count = actions.shape[1]
    score_scale = HD ** (-0.5)
    full_inputs = lax.all_gather(hidden_in, "tensor", axis=3, tiled=True)
    full_grads = lax.all_gather(out_grad, "tensor", axis=3, tiled=True)
    input_rows = full_inputs.reshape(row_count, model_width)
    grad_rows = full_grads.reshape(row_count, model_width)
    own_cache = clean_cache[0]
    nearer = from_behind(own_cache, TM, 1)
    farther = from_behind(own_cache, TM, 2)
    reach = offsets[0]
    allowed = jnp.concatenate(
        [
            jnp.full((tokens_here,), reach >= 2),
            jnp.full((tokens_here,), reach >= 1),
            jnp.ones((tokens_here,), bool),
        ]
    )
    block_shape = (steps_here, tokens_here, head_width)
    key_block = jnp.concatenate(
        [
            jnp.broadcast_to(farther[0], block_shape),
            jnp.broadcast_to(nearer[0], block_shape),
            noisy_keys[0],
        ],
        axis=1,
    )
    value_block = jnp.concatenate(
        [
            jnp.broadcast_to(farther[1], block_shape),
            jnp.broadcast_to(nearer[1], block_shape),
            noisy_values[0],
        ],
        axis=1,
    )
    query_heads = noisy_queries[0].reshape(steps_here, tokens_here, heads_here, HD)
    key_heads = key_block.reshape(steps_here, 3 * tokens_here, heads_here, HD)
    value_heads = value_block.reshape(steps_here, 3 * tokens_here, heads_here, HD)
    scores = (
        jnp.einsum("sqhe,skhe->shqk", query_heads, key_heads, preferred_element_type=jnp.float32)
        * score_scale
    )
    masked = jnp.where(allowed[None, None, None, :], scores, -1e30)
    largest = jnp.max(masked, axis=-1, keepdims=True)
    raised = jnp.exp(masked - largest)
    probs = raised / jnp.sum(raised, axis=-1, keepdims=True)
    probs_low = probs.astype(jnp.bfloat16)
    attended = (
        jnp.einsum("shqk,skhe->sqhe", probs_low, value_heads, preferred_element_type=jnp.float32)
        .astype(jnp.bfloat16)
        .reshape(row_count, head_width)
    )
    onehot = (actions[0][:, None] == jnp.arange(action_table.shape[0])[None, :]).astype(
        jnp.bfloat16
    )
    action_rows = jnp.dot(onehot, action_table, preferred_element_type=jnp.float32)
    branch_width = branch_in.shape[1]
    pre_act = (
        jnp.dot(input_rows, branch_in, preferred_element_type=jnp.float32).reshape(
            steps_here, action_count, tokens_here // action_count, branch_width
        )
        + action_rows[None, :, None, :]
    )
    pre_act = pre_act.reshape(row_count, branch_width)
    branch_act = gelu_value(pre_act).astype(jnp.bfloat16)
    group_count = lax.axis_size("tensor")
    group_width = model_width // group_count
    partial_value = jnp.einsum(
        "rk,kjn->jrn",
        attended,
        out_proj.reshape(-1, group_count, group_width),
        preferred_element_type=jnp.float32,
    ) + jnp.einsum(
        "rk,kjn->jrn",
        branch_act,
        branch_out.reshape(-1, group_count, group_width),
        preferred_element_type=jnp.float32,
    )
    attended_grad = contract_cols(grad_rows, out_proj).astype(jnp.bfloat16)
    pre_grad = (contract_cols(grad_rows, branch_out) * gelu_slope(pre_act)).astype(jnp.bfloat16)
    tm_count = lax.axis_size(TM)
    grouped = jnp.sum(
        pre_grad.reshape(
            steps_here, action_count, tokens_here // action_count, branch_width
        ).astype(jnp.float32),
        axis=(0, 2),
    )
    table_term = jnp.dot(onehot.astype(jnp.float32).T, grouped, precision=lax.Precision.HIGHEST)
    head_cols = attended.shape[1]
    input_side = jnp.concatenate(
        [jnp.zeros((row_count, head_cols + branch_width), jnp.bfloat16), pre_grad], axis=1
    )
    grad_side = jnp.concatenate(
        [attended, branch_act, jnp.zeros((row_count, branch_width), jnp.bfloat16)], axis=1
    )
    terms = contract_rows(
        jnp.concatenate([input_rows, grad_rows], axis=0),
        jnp.concatenate([input_side, grad_side], axis=0),
    ).astype(jnp.bfloat16)
    merged = two_stage_scatter(terms).astype(jnp.float32)
    table_blocks = lax.all_to_all(
        table_term.astype(jnp.bfloat16).reshape(tm_count, -1, branch_width), TM, 0, 0, tiled=True
    )
    summed = (
        merged[:, :head_cols].T,
        merged[:, head_cols + branch_width :],
        merged[:, head_cols : head_cols + branch_width].T,
        jnp.sum(table_blocks.astype(jnp.float32), axis=0),
    )
    input_term = jnp.einsum(
        "rk,jnk->jrn",
        pre_grad,
        branch_in.reshape(group_count, group_width, -1),
        preferred_element_type=jnp.float32,
    )
    layer_sum, input_sum = jnp.split(
        sum_over_groups(
            jnp.concatenate([partial_value, input_term], axis=1).astype(jnp.bfloat16),
            2 * steps_here,
            tokens_here,
        ),
        2,
        axis=1,
    )
    layer_out = (hidden_in.astype(jnp.float32) + layer_sum).astype(jnp.bfloat16)
    input_grad = (out_grad.astype(jnp.float32) + input_sum).astype(jnp.bfloat16)
    weight_grads = (summed, input_grad)
    grad_heads = attended_grad.reshape(steps_here, tokens_here, heads_here, HD)
    value_all = jnp.einsum(
        "shqk,sqhe->skhe", probs_low, grad_heads, preferred_element_type=jnp.float32
    )
    prob_grad = jnp.einsum(
        "sqhe,skhe->shqk", grad_heads, value_heads, preferred_element_type=jnp.float32
    )
    centre = jnp.sum(prob_grad * probs, axis=-1, keepdims=True)
    score_grad = (probs * (prob_grad - centre) * score_scale).astype(jnp.bfloat16)
    query_grad = (
        jnp.einsum("shqk,skhe->sqhe", score_grad, key_heads, preferred_element_type=jnp.float32)
        .astype(jnp.bfloat16)
        .reshape(1, steps_here, tokens_here, head_width)
    )
    key_all = jnp.einsum(
        "shqk,sqhe->skhe", score_grad, query_heads, preferred_element_type=jnp.float32
    ).reshape(steps_here, 3 * tokens_here, head_width)
    value_all = value_all.reshape(steps_here, 3 * tokens_here, head_width)
    own_key = key_all[:, 2 * tokens_here :].astype(jnp.bfloat16)[None]
    own_value = value_all[:, 2 * tokens_here :].astype(jnp.bfloat16)[None]
    toward_far = jnp.stack(
        [jnp.sum(key_all[:, :tokens_here], axis=0), jnp.sum(value_all[:, :tokens_here], axis=0)]
    )
    toward_near = jnp.stack(
        [
            jnp.sum(key_all[:, tokens_here : 2 * tokens_here], axis=0),
            jnp.sum(value_all[:, tokens_here : 2 * tokens_here], axis=0),
        ]
    )
    from_next = from_behind(toward_near.astype(jnp.bfloat16), TM, -1).astype(toward_near.dtype)
    from_after = from_behind(toward_far.astype(jnp.bfloat16), TM, -2).astype(toward_far.dtype)
    received = from_next + from_after
    attention_grads = (query_grad, own_key, own_value, received[None])
    summed, input_grad = weight_grads
    query_grad, own_key, own_value, cache_grad = attention_grads
    return (
        layer_out,
        input_grad,
        query_grad,
        own_key,
        own_value,
        cache_grad,
        summed[0],
        summed[1],
        summed[2],
        summed[3],
    )


def solution(mesh):
    in_specs = (
        P("tm", None, None, "tensor"),
        P("tm", None, None, "tensor"),
        P("tm", None, None, "tensor"),
        P("tm", None, None, "tensor"),
        P("tm", None, None, "tensor"),
        P("tensor", None),
        P(None, "tensor"),
        P("tensor", None),
        P(None, "tensor"),
        P("tm", None),
        P("tm"),
        P("tm", None, None, "tensor"),
    )
    out_specs = (
        P("tm", None, None, "tensor"),
        P("tm", None, None, "tensor"),
        P("tm", None, None, "tensor"),
        P("tm", None, None, "tensor"),
        P("tm", None, None, "tensor"),
        P("tm", None, None, "tensor"),
        P("tensor", "tm"),
        P("tm", "tensor"),
        P("tensor", "tm"),
        P("tm", "tensor"),
    )
    shape = mesh.devices.shape
    inner = jax.sharding.Mesh(
        mesh.devices.reshape(shape[0] // 2, 2, shape[1]), ("tmo", "core", "tensor")
    )
    swap = lambda spec: P(*[TM if part == "tm" else part for part in spec])
    return jax.shard_map(
        body,
        mesh=inner,
        in_specs=tuple(swap(s) for s in in_specs),
        out_specs=tuple(swap(s) for s in out_specs),
        check_vma=False,
    )
```
